512 devices in a mesh: rep: 8 (over y_lo, core), seq: 2 (over y_hi), tp: 32 (over x, z).
Axes of the slice: x: 4, y: 8 (y_hi: 2, y_lo: 4; y = y_hi * 4 + y_lo), z: 8, core: 2. Of those that a mesh axis runs over, the one named last changes fastest.
Arguments:
- hidden: bfloat16 [3072, 8192], P('rep', ('seq', 'tp')), may hold values from -100 to 100
- gain: float32 [8192], replicated, may hold values from 0.1 to 1.9
- w_query: bfloat16 [8192, 8192], P('seq', 'tp'), may hold values from -1 to 1
- w_keyval: bfloat16 [2, 4096, 2048], P(None, 'tp'), may hold values from -1 to 1
- lengths: int32 [8, 2], replicated, may hold values from 128 to 192, as said below
- routes: int32 [8, 2], replicated, may hold values from 0 to 7, as said below
Outputs:
- attended: bfloat16 [3072, 8192], P(('rep', 'seq'), 'tp')
The draws below stay inside these ranges and needn't reach their ends.
Inputs may be any that keep to these rules, and one draw needn't show every extreme that they name: `routes`: for each j, the responses j of the 8 rollout groups go to 8 different replicas, so each replica receives exactly 2 responses. `lengths`: the responses that one rollout group sends to one replica hold at most 192 tokens together, and in every draw some group sends exactly 192 tokens to one replica.
All inputs are finite; a program needn't handle non-finite values.
Results may differ from the reference program's by a relative error of at most 0.0076.
Values may be sent and summed in bfloat16 or wider, within the bound.
No kernel may reach another device: no remote copies, remote signals or barrier semaphores. Data moves between devices by JAX's collectives and lax.ppermute only.
A program may use at most 64 MiB of HBM per device.

```python
import math
import jax
import jax.numpy as jnp
from jax import lax

D = 8192
QH = 64
KVH = 8
HD = 128
RESP = 2
LMAX = 192
LMIN = 128
GROUPS = 8
DSPLIT = 2
BUFFER = 384


def draw_hidden(key, part):
    row_count = GROUPS * BUFFER
    values = jax.random.normal(jax.random.fold_in(key, 1), (row_count, D), jnp.float32)
    return jnp.clip(values, -6.0, 6.0).astype(jnp.bfloat16)


def draw_w_query(key, part):
    base = jnp.clip(jax.random.normal(jax.random.fold_in(key, 21), (D, QH * HD), jnp.float32), -6.0, 6.0) / math.sqrt(D)
    return base.astype(jnp.bfloat16)


def draw_w_keyval(key, part):
    base = jnp.clip(jax.random.normal(jax.random.fold_in(key, 22), (D, 2 * KVH * HD), jnp.float32), -6.0, 6.0) / math.sqrt(D)
    return base.reshape(DSPLIT, D // DSPLIT, 2 * KVH * HD).astype(jnp.bfloat16)


def routing_plan(key):
    base_key = jax.random.fold_in(key, 31)
    order = jax.random.permutation(jax.random.fold_in(base_key, 5), RESP).astype(jnp.int32)
    group_ids = jnp.arange(GROUPS, dtype=jnp.int32)
    route_table = (group_ids[:, None] + GROUPS // 2 + order[None, :]) % GROUPS
    length_table = jax.random.randint(jax.random.fold_in(base_key, 3), (GROUPS, RESP), LMIN, LMAX + 1)
    chosen = jax.random.randint(jax.random.fold_in(base_key, 4), (), 0, GROUPS)
    full_rows = (group_ids[:, None] == chosen) & (order[None, :] % GROUPS == 0)
    length_table = jnp.where(full_rows, LMAX, length_table)
    return (length_table.astype(jnp.int32), route_table.astype(jnp.int32))


def draw_lengths(key, part):
    return routing_plan(key)[0]


def draw_routes(key, part):
    return routing_plan(key)[1]


def setup_inputs(seed: int = 0) -> dict:
    splits = jax.random.split(jax.random.key(seed), 7)
    return {
        "hidden": draw_hidden(jax.random.fold_in(splits[6], 71), 0),
        "gain": jnp.clip(1.0 + 0.18 * jax.random.normal(splits[1], (D,), jnp.float32), 0.1, 1.9),
        "w_query": draw_w_query(jax.random.fold_in(splits[6], 71), 0),
        "w_keyval": draw_w_keyval(jax.random.fold_in(splits[6], 71), 0),
        "lengths": draw_lengths(jax.random.fold_in(splits[6], 71), 0),
        "routes": draw_routes(jax.random.fold_in(splits[6], 71), 0),
    }


ROPE_BASE = 500000.0
NORM_EPS = 1e-05
MASK_FILL = -1e+30

def response_tables(lengths, routes):
    flat_len = lengths.reshape(-1).astype(jnp.int32)
    flat_route = routes.reshape(-1).astype(jnp.int32)
    response_ids = jnp.arange(flat_len.shape[0], dtype=jnp.int32)
    group_of = response_ids // RESP
    same_route = flat_route[:, None] == flat_route[None, :]
    same_group = group_of[:, None] == group_of[None, :]
    earlier = response_ids[None, :] < response_ids[:, None]
    dest_off = lax.optimization_barrier(jnp.sum(jnp.where(same_route & earlier, flat_len[None, :], 0), axis=1)).astype(jnp.int32)
    pair_off = lax.optimization_barrier(jnp.sum(jnp.where(same_route & same_group & earlier, flat_len[None, :], 0), axis=1)).astype(jnp.int32)
    src_start = lax.optimization_barrier(jnp.sum(jnp.where(same_group & earlier, flat_len[None, :], 0), axis=1)).astype(jnp.int32)
    return (flat_len, flat_route, group_of, dest_off, pair_off, src_start)

def locate(positions, replica, tables):
    flat_len, flat_route, group_of, dest_off, pair_off, src_start = tables
    response_ids = jnp.arange(flat_len.shape[0], dtype=jnp.int32)
    position_col = positions[:, None]
    inside = (flat_route[None, :] == replica) & (dest_off[None, :] <= position_col) & (position_col < dest_off[None, :] + flat_len[None, :])
    inside_int = inside.astype(jnp.int32)
    segment = lax.optimization_barrier(jnp.sum(inside_int * (response_ids[None, :] + 1), axis=1)) - 1
    seg_start = lax.optimization_barrier(jnp.sum(inside_int * dest_off[None, :], axis=1))
    source_group = lax.optimization_barrier(jnp.sum(inside_int * group_of[None, :], axis=1))
    pair_first = lax.optimization_barrier(jnp.sum(inside_int * (dest_off - pair_off)[None, :], axis=1))
    source = lax.optimization_barrier(jnp.sum(inside_int * src_start[None, :], axis=1))
    within = jnp.where(segment >= 0, positions - seg_start, 0).astype(jnp.int32)
    return (segment, within, source_group, pair_first, source)

def rotary(values_in, within):
    head_dim = values_in.shape[-1]
    half_dim = head_dim // 2
    freq_index = jnp.arange(half_dim, dtype=jnp.float32)
    inverse = jnp.power(ROPE_BASE, -2.0 * freq_index / head_dim)
    angles = within.astype(jnp.float32)[:, None] * inverse[None, :]
    cosine = jnp.cos(angles)[:, None, :]
    sine_part = jnp.sin(angles)[:, None, :]
    lower_half = values_in[..., :half_dim]
    upper_half = values_in[..., half_dim:]
    return jnp.concatenate([lower_half * cosine - upper_half * sine_part, upper_half * cosine + lower_half * sine_part], axis=-1)

def reference(hidden, gain, w_query, w_keyval, lengths, routes):
    tables = response_tables(lengths, routes)
    w_keys = w_keyval.reshape(D, 2 * KVH * HD)
    positions = jnp.arange(BUFFER, dtype=jnp.int32)
    score_scale = 1.0 / math.sqrt(HD)

    def one_replica(replica):
        segment, within, source_group, pair_first, source = locate(positions, replica, tables)
        valid = segment >= 0
        src_row = jnp.where(valid, source_group * BUFFER + source + within, 0).astype(jnp.int32)
        packed = jnp.where(valid[:, None], jnp.take(hidden, src_row, axis=0), jnp.zeros((), hidden.dtype))
        packed_f = packed.astype(jnp.float32)
        inverse_rms = lax.rsqrt(lax.optimization_barrier(jnp.sum(packed_f * packed_f, axis=1)) / D + NORM_EPS)
        scaled = (packed_f * gain[None, :]).astype(jnp.bfloat16)
        query_raw = jnp.dot(scaled, w_query, preferred_element_type=jnp.float32)
        keyval_raw = jnp.dot(scaled, w_keys, preferred_element_type=jnp.float32).reshape(BUFFER, KVH, 2, HD)
        queries = rotary(inverse_rms[:, None, None] * query_raw.reshape(BUFFER, QH, HD), within).astype(jnp.bfloat16)
        keys = rotary(inverse_rms[:, None, None] * keyval_raw[:, :, 0], within).astype(jnp.bfloat16)
        values = (inverse_rms[:, None, None] * keyval_raw[:, :, 1]).astype(jnp.bfloat16)
        allowed = (segment[None, :] == segment[:, None]) & valid[:, None] & (positions[None, :] <= positions[:, None]) | (positions[None, :] == positions[:, None])
        grouped_q = queries.reshape(BUFFER, KVH, QH // KVH, HD).transpose(1, 0, 2, 3)

        def one_head(operands):
            query_block, key_block, value_block = operands
            scores = jnp.einsum('pgd,kd->pgk', query_block.astype(jnp.float32), key_block.astype(jnp.float32)) * score_scale
            scores = jnp.where(allowed[:, None, :], scores, MASK_FILL)
            largest = lax.optimization_barrier(jnp.max(scores, axis=2, keepdims=True))
            exp_terms = jnp.where(allowed[:, None, :], jnp.exp(scores - largest), 0.0)
            denominator = lax.optimization_barrier(jnp.sum(exp_terms, axis=2))
            rounded = lax.optimization_barrier(exp_terms.astype(jnp.bfloat16)).astype(jnp.float32)
            mixed_sum = jnp.einsum('pgk,kd->pgd', rounded, value_block.astype(jnp.float32))
            return mixed_sum / denominator[..., None]
        heads_out = lax.map(one_head, (grouped_q, keys.transpose(1, 0, 2), values.transpose(1, 0, 2)))
        attended = heads_out.transpose(1, 0, 2, 3).reshape(BUFFER, QH * HD).astype(jnp.bfloat16)
        return jnp.where(valid[:, None], attended, jnp.zeros((), jnp.bfloat16))
    outputs = lax.map(one_replica, jnp.arange(GROUPS, dtype=jnp.int32))
    return outputs.reshape(GROUPS * BUFFER, QH * HD)
```

```python
import math

import jax
import jax.numpy as jnp
from jax import lax
from jax.sharding import PartitionSpec as P

D = 8192
QH = 64
KVH = 8
HD = 128
RESP = 2
LMAX = 192
BUFFER = 384


ROPE_BASE = 500000.0
NORM_EPS = 1e-05
MASK_FILL = -1e30


def response_tables(lengths, routes):
    flat_len = lengths.reshape(-1)
    flat_route = routes.reshape(-1)
    response_ids = jnp.arange(flat_len.shape[0], dtype=jnp.int32)
    group_of = response_ids // RESP
    same_route = flat_route[:, None] == flat_route[None, :]
    same_group = group_of[:, None] == group_of[None, :]
    earlier = response_ids[None, :] < response_ids[:, None]
    dest_off = jnp.sum(jnp.where(same_route & earlier, flat_len[None, :], 0), axis=1)
    pair_off = jnp.sum(jnp.where(same_route & same_group & earlier, flat_len[None, :], 0), axis=1)
    src_start = jnp.sum(jnp.where(same_group & earlier, flat_len[None, :], 0), axis=1)
    return (flat_len, flat_route, group_of, dest_off, pair_off, src_start)


def locate(positions, replica, tables):
    flat_len, flat_route, group_of, dest_off, pair_off, src_start = tables
    response_ids = jnp.arange(flat_len.shape[0], dtype=jnp.int32)
    position_col = positions[:, None]
    inside = (
        (flat_route[None, :] == replica)
        & (dest_off[None, :] <= position_col)
        & (position_col < dest_off[None, :] + flat_len[None, :])
    )
    inside_int = inside.astype(jnp.int32)
    segment = jnp.sum(inside_int * (response_ids[None, :] + 1), axis=1) - 1
    seg_start = jnp.sum(inside_int * dest_off[None, :], axis=1)
    source_group = jnp.sum(inside_int * group_of[None, :], axis=1)
    pair_first = jnp.sum(inside_int * (dest_off - pair_off)[None, :], axis=1)
    source = jnp.sum(inside_int * src_start[None, :], axis=1)
    within = jnp.where(segment >= 0, positions - seg_start, 0)
    return (segment, within, source_group, pair_first, source)


def rotary(values_in, within):
    head_dim = values_in.shape[-1]
    half_dim = head_dim // 2
    freq_index = jnp.arange(half_dim, dtype=jnp.float32)
    inverse = jnp.power(ROPE_BASE, -2.0 * freq_index / head_dim)
    angles = within.astype(jnp.float32)[:, None] * inverse[None, :]
    cosine = jnp.cos(angles)[:, None, :]
    sine_part = jnp.sin(angles)[:, None, :]
    lower_half = values_in[..., :half_dim]
    upper_half = values_in[..., half_dim:]
    return jnp.concatenate(
        [
            lower_half * cosine - upper_half * sine_part,
            upper_half * cosine + lower_half * sine_part,
        ],
        axis=-1,
    )


def fill_rows(table, indices, present):
    taken = jnp.take(table, indices.reshape(-1), axis=0)
    return jnp.where(present.reshape(-1)[:, None], taken, jnp.zeros((), table.dtype))


def local(hidden, gain, w_query, w_keyval, lengths, routes):
    rep_count = lax.axis_size("rep")
    seq_count = lax.axis_size("seq")
    group_size = lax.axis_size("tu")
    tp_count = lax.axis_size("tg") * group_size
    replica = lax.axis_index("rep")
    seq_index = lax.axis_index("seq")
    sub = lax.axis_index("tu")
    feature_cols = hidden.shape[1]
    local_rows = BUFFER // seq_count
    capacity = (RESP + rep_count - 1) // rep_count * LMAX
    head_count = w_query.shape[1] // HD
    kv_cols = 2 * HD // group_size
    quarter = HD // 4

    tables = response_tables(lengths, routes)
    flat_len, flat_route, group_of, dest_off, pair_off, src_start = tables
    my_len = lax.dynamic_slice_in_dim(flat_len, replica * RESP, RESP)
    my_route = lax.dynamic_slice_in_dim(flat_route, replica * RESP, RESP)
    my_pair = lax.dynamic_slice_in_dim(pair_off, replica * RESP, RESP)
    my_start = lax.dynamic_slice_in_dim(src_start, replica * RESP, RESP)
    slot_ids = jnp.arange(capacity, dtype=jnp.int32)
    targets = jnp.arange(rep_count, dtype=jnp.int32)
    offsets = jnp.broadcast_to(slot_ids[None, :], (rep_count, capacity))[:, :, None]
    inside = (
        (my_route[None, None, :] == targets[:, None, None])
        & (my_pair[None, None, :] <= offsets)
        & (offsets < (my_pair + my_len)[None, None, :])
    )
    inside_int = inside.astype(jnp.int32)
    src_rows = jnp.sum(
        inside_int * (my_start[None, None, :] + offsets - my_pair[None, None, :]), axis=2
    )
    present = jnp.any(inside, axis=2)
    outgoing = fill_rows(hidden, src_rows, present)
    incoming = lax.all_to_all(outgoing, "rep", split_axis=0, concat_axis=0, tiled=True)
    all_pos = jnp.arange(BUFFER, dtype=jnp.int32)
    segment, within, source_group, pair_first, source = locate(all_pos, replica, tables)
    valid = segment >= 0
    gathered_idx = jnp.where(valid, source_group * capacity + all_pos - pair_first, 0)
    assembled = fill_rows(incoming, gathered_idx, valid)

    w_half = lax.dynamic_index_in_dim(w_keyval, seq_index, 0, keepdims=False)
    w_half = w_half.reshape(feature_cols, KVH, 2, 2, 2, quarter)
    w_half = w_half.transpose(1, 2, 4, 0, 3, 5).reshape(tp_count, feature_cols, kv_cols)
    w_kv = lax.all_to_all(w_half, ("tg", "tu"), split_axis=0, concat_axis=0, tiled=True)

    gathered = lax.all_gather(assembled, ("tg", "tu"), axis=0, tiled=False)
    gain_half = lax.dynamic_index_in_dim(
        gain.reshape(seq_count, tp_count, feature_cols), seq_index, 0, keepdims=False
    )
    gathered_f = gathered.astype(jnp.float32)
    scaled = (gathered_f * gain_half[:, None, :]).astype(jnp.bfloat16)
    squares = jnp.sum(gathered_f * gathered_f, axis=(0, 2))
    w_q = w_query.reshape(tp_count, feature_cols, w_query.shape[1])
    query_part = jnp.einsum("tri,tic->rc", scaled, w_q, preferred_element_type=jnp.float32)
    kv_part = jnp.einsum("tri,tic->rc", scaled, w_kv, preferred_element_type=jnp.float32)

    query_halves = query_part.reshape(seq_count, local_rows, query_part.shape[1])
    partner = seq_count - 1 - seq_index
    to_partner = lax.dynamic_index_in_dim(query_halves, partner, 0, keepdims=False)
    got_query, got_kv, got_squares = lax.ppermute(
        (to_partner, kv_part, squares), "seq", perm=[(0, 1), (1, 0)]
    )
    query_raw = lax.dynamic_index_in_dim(query_halves, seq_index, 0, keepdims=False) + got_query
    kv_raw = kv_part + got_kv
    inverse_rms = lax.rsqrt((squares + got_squares) / D + NORM_EPS)

    query_pos = seq_index * local_rows + jnp.arange(local_rows, dtype=jnp.int32)
    query_seg = lax.dynamic_slice_in_dim(segment, seq_index * local_rows, local_rows)
    query_within = lax.dynamic_slice_in_dim(within, seq_index * local_rows, local_rows)
    query_rms = lax.dynamic_slice_in_dim(inverse_rms, seq_index * local_rows, local_rows)
    query_valid = query_seg >= 0
    queries = rotary(
        query_rms[:, None, None] * query_raw.reshape(local_rows, head_count, HD), query_within
    ).astype(jnp.bfloat16)

    kv_scaled = (inverse_rms[:, None] * kv_raw).reshape(BUFFER, 2, quarter)
    freq_index = (sub % 2 * quarter + jnp.arange(quarter, dtype=jnp.int32)).astype(jnp.float32)
    inverse = jnp.power(ROPE_BASE, -2.0 * freq_index / HD)
    angles = within.astype(jnp.float32)[:, None] * inverse[None, :]
    cosine = jnp.cos(angles)
    sine_part = jnp.sin(angles)
    lower_half = kv_scaled[:, 0]
    upper_half = kv_scaled[:, 1]
    roped = jnp.stack(
        [lower_half * cosine - upper_half * sine_part, upper_half * cosine + lower_half * sine_part],
        axis=1,
    )
    piece = jnp.where(sub < 2, roped, kv_scaled).astype(jnp.bfloat16)
    pieces = lax.all_gather(piece, "tu", axis=0, tiled=False)
    pieces = pieces.reshape(2, 2, BUFFER, 2, quarter).transpose(0, 2, 3, 1, 4)
    key_part = pieces[0].reshape(BUFFER, HD)
    value_part = pieces[1].reshape(BUFFER, HD)

    score_scale = 1.0 / math.sqrt(HD)
    key_pos = all_pos
    allowed = (segment[None, :] == query_seg[:, None]) & query_valid[:, None] & (
        key_pos[None, :] <= query_pos[:, None]
    ) | (key_pos[None, :] == query_pos[:, None])
    scores = (
        jnp.einsum("rhd,kd->rhk", queries, key_part, preferred_element_type=jnp.float32)
        * score_scale
    )
    scores = jnp.where(allowed[:, None, :], scores, MASK_FILL)
    new_max = jnp.max(scores, axis=2)
    prob_terms = jnp.where(allowed[:, None, :], jnp.exp(scores - new_max[:, :, None]), 0.0)
    totals = jnp.sum(prob_terms, axis=2)
    accum = jnp.einsum(
        "rhk,kd->rhd",
        prob_terms.astype(jnp.bfloat16),
        value_part,
        preferred_element_type=jnp.float32,
    )
    attended = (
        (accum / totals[:, :, None]).reshape(local_rows, head_count * HD).astype(jnp.bfloat16)
    )
    return jnp.where(query_valid[:, None], attended, jnp.zeros((), jnp.bfloat16))


def solution(mesh):
    heads_per_kv = QH // KVH
    tp_count = mesh.shape["tp"]
    group_size = heads_per_kv * tp_count // QH
    devices = mesh.devices.reshape(
        mesh.shape["rep"], mesh.shape["seq"], tp_count // group_size, group_size
    )
    grid = jax.sharding.Mesh(devices, ("rep", "seq", "tg", "tu"))
    tp = ("tg", "tu")
    in_specs = (
        P("rep", ("seq",) + tp),
        P(),
        P("seq", tp),
        P(None, tp, None),
        P(),
        P(),
    )
    out_specs = P(("rep", "seq"), tp)
    return jax.shard_map(local, mesh=grid, in_specs=in_specs, out_specs=out_specs, check_vma=False)
```

```python
import math

import jax
import jax.numpy as jnp
from jax import lax
from jax.sharding import PartitionSpec as P

D = 8192
QH = 64
KVH = 8
HD = 128
RESP = 2
LMAX = 192
BUFFER = 384


ROPE_BASE = 500000.0
NORM_EPS = 1e-05
MASK_FILL = -1e30


def response_tables(lengths, routes):
    flat_len = lengths.reshape(-1)
    flat_route = routes.reshape(-1)
    response_ids = jnp.arange(flat_len.shape[0], dtype=jnp.int32)
    group_of = response_ids // RESP
    same_route = flat_route[:, None] == flat_route[None, :]
    same_group = group_of[:, None] == group_of[None, :]
    earlier = response_ids[None, :] < response_ids[:, None]
    dest_off = jnp.sum(jnp.where(same_route & earlier, flat_len[None, :], 0), axis=1)
    pair_off = jnp.sum(jnp.where(same_route & same_group & earlier, flat_len[None, :], 0), axis=1)
    src_start = jnp.sum(jnp.where(same_group & earlier, flat_len[None, :], 0), axis=1)
    return (flat_len, flat_route, group_of, dest_off, pair_off, src_start)


def locate(positions, replica, tables):
    flat_len, flat_route, group_of, dest_off, pair_off, src_start = tables
    response_ids = jnp.arange(flat_len.shape[0], dtype=jnp.int32)
    position_col = positions[:, None]
    inside = (
        (flat_route[None, :] == replica)
        & (dest_off[None, :] <= position_col)
        & (position_col < dest_off[None, :] + flat_len[None, :])
    )
    inside_int = inside.astype(jnp.int32)
    segment = jnp.sum(inside_int * (response_ids[None, :] + 1), axis=1) - 1
    seg_start = jnp.sum(inside_int * dest_off[None, :], axis=1)
    source_group = jnp.sum(inside_int * group_of[None, :], axis=1)
    pair_first = jnp.sum(inside_int * (dest_off - pair_off)[None, :], axis=1)
    source = jnp.sum(inside_int * src_start[None, :], axis=1)
    within = jnp.where(segment >= 0, positions - seg_start, 0)
    return (segment, within, source_group, pair_first, source)


def rotary(values_in, within):
    head_dim = values_in.shape[-1]
    half_dim = head_dim // 2
    freq_index = jnp.arange(half_dim, dtype=jnp.float32)
    inverse = jnp.power(ROPE_BASE, -2.0 * freq_index / head_dim)
    angles = within.astype(jnp.float32)[:, None] * inverse[None, :]
    cosine = jnp.cos(angles)[:, None, :]
    sine_part = jnp.sin(angles)[:, None, :]
    lower_half = values_in[..., :half_dim]
    upper_half = values_in[..., half_dim:]
    return jnp.concatenate(
        [
            lower_half * cosine - upper_half * sine_part,
            upper_half * cosine + lower_half * sine_part,
        ],
        axis=-1,
    )


def fill_rows(table, indices, present):
    taken = jnp.take(table, indices.reshape(-1), axis=0)
    return jnp.where(present.reshape(-1)[:, None], taken, jnp.zeros((), table.dtype))


def local(hidden, gain, w_query, w_keyval, lengths, routes):
    rep_count = lax.axis_size("rep")
    seq_count = lax.axis_size("seq")
    x_count = lax.axis_size("x")
    group_size = lax.axis_size("zl")
    z_count = lax.axis_size("zh") * group_size
    tp_count = x_count * z_count
    replica = lax.axis_index("rep")
    seq_index = lax.axis_index("seq")
    sub = lax.axis_index("zl")
    feature_cols = hidden.shape[1]
    local_rows = BUFFER // seq_count
    head_count = w_query.shape[1] // HD
    kv_cols = 2 * HD // group_size
    quarter = HD // 4

    tables = response_tables(lengths, routes)
    flat_len, flat_route, group_of, dest_off, pair_off, src_start = tables
    my_route = lax.dynamic_slice_in_dim(flat_route, replica * RESP, RESP)
    my_start = lax.dynamic_slice_in_dim(src_start, replica * RESP, RESP)
    first_block = lax.dynamic_slice_in_dim(hidden, my_start[0], LMAX, 0)
    second_block = lax.dynamic_slice_in_dim(hidden, my_start[1], LMAX, 0)
    targets = jnp.arange(rep_count, dtype=jnp.int32)
    outgoing = jnp.where(
        (targets == my_route[0])[:, None, None], first_block[None], second_block[None]
    ).reshape(rep_count * LMAX, feature_cols)
    incoming = lax.all_to_all(outgoing, "rep", split_axis=0, concat_axis=0, tiled=True)
    all_pos = jnp.arange(BUFFER, dtype=jnp.int32)
    segment, within, source_group, pair_first, source = locate(all_pos, replica, tables)
    valid = segment >= 0
    gathered_idx = jnp.where(valid, source_group * LMAX + all_pos - pair_first, 0)
    assembled = fill_rows(incoming, gathered_idx, valid)

    w_half = lax.dynamic_index_in_dim(w_keyval, seq_index, 0, keepdims=False)
    w_half = w_half.reshape(feature_cols, KVH, 2, 2, 2, quarter)
    w_half = w_half.transpose(1, 2, 4, 0, 3, 5).reshape(tp_count, feature_cols, kv_cols)
    w_kv = lax.all_to_all(w_half, ("x", "zh", "zl"), split_axis=0, concat_axis=0, tiled=True)
    w_kv = w_kv.reshape(x_count, z_count, feature_cols, kv_cols)

    gathered = lax.all_gather(assembled, "x", axis=0, tiled=False)
    gathered = lax.all_gather(gathered, ("zh", "zl"), axis=0, tiled=False)
    gain_half = lax.dynamic_index_in_dim(
        gain.reshape(seq_count, x_count, z_count, feature_cols), seq_index, 0, keepdims=False
    )
    gathered_f = gathered.astype(jnp.float32)
    scaled = (gathered_f * gain_half.transpose(1, 0, 2)[:, :, None, :]).astype(jnp.bfloat16)
    squares = jnp.sum(gathered_f * gathered_f, axis=(0, 1, 3))
    w_q = w_query.reshape(x_count, z_count, feature_cols, w_query.shape[1])
    query_part = jnp.einsum("zxri,xzic->rc", scaled, w_q, preferred_element_type=jnp.float32)
    kv_part = jnp.einsum("zxri,xzic->rc", scaled, w_kv, preferred_element_type=jnp.float32)

    query_halves = query_part.reshape(seq_count, local_rows, query_part.shape[1])
    partner = seq_count - 1 - seq_index
    to_partner = lax.dynamic_index_in_dim(query_halves, partner, 0, keepdims=False)
    kv_rows = kv_part.reshape(seq_count, local_rows, kv_cols).transpose(1, 0, 2)
    square_rows = squares.reshape(seq_count, local_rows).transpose(1, 0)
    payload = jnp.concatenate(
        [to_partner, kv_rows.reshape(local_rows, -1), square_rows], axis=1
    )
    got = lax.ppermute(payload, "seq", perm=[(0, 1), (1, 0)])
    query_cols = query_part.shape[1]
    kv_width = seq_count * kv_cols
    got_query = got[:, :query_cols]
    got_kv = got[:, query_cols : query_cols + kv_width].reshape(local_rows, seq_count, kv_cols)
    got_kv = got_kv.transpose(1, 0, 2).reshape(BUFFER, kv_cols)
    got_squares = got[:, query_cols + kv_width :].transpose(1, 0).reshape(BUFFER)
    query_raw = lax.dynamic_index_in_dim(query_halves, seq_index, 0, keepdims=False) + got_query
    kv_raw = kv_part + got_kv
    inverse_rms = lax.rsqrt((squares + got_squares) / D + NORM_EPS)

    query_pos = seq_index * local_rows + jnp.arange(local_rows, dtype=jnp.int32)
    query_seg = lax.dynamic_slice_in_dim(segment, seq_index * local_rows, local_rows)
    query_within = lax.dynamic_slice_in_dim(within, seq_index * local_rows, local_rows)
    query_rms = lax.dynamic_slice_in_dim(inverse_rms, seq_index * local_rows, local_rows)
    query_valid = query_seg >= 0
    queries = rotary(
        query_rms[:, None, None] * query_raw.reshape(local_rows, head_count, HD), query_within
    ).astype(jnp.bfloat16)

    kv_scaled = (inverse_rms[:, None] * kv_raw).reshape(BUFFER, 2, quarter)
    freq_index = (sub % 2 * quarter + jnp.arange(quarter, dtype=jnp.int32)).astype(jnp.float32)
    inverse = jnp.power(ROPE_BASE, -2.0 * freq_index / HD)
    angles = within.astype(jnp.float32)[:, None] * inverse[None, :]
    cosine = jnp.cos(angles)
    sine_part = jnp.sin(angles)
    lower_half = kv_scaled[:, 0]
    upper_half = kv_scaled[:, 1]
    roped = jnp.stack(
        [lower_half * cosine - upper_half * sine_part, upper_half * cosine + lower_half * sine_part],
        axis=1,
    )
    piece = jnp.where(sub < 2, roped, kv_scaled).astype(jnp.bfloat16)
    shifted = [piece] + [
        lax.ppermute(piece, "zl", perm=[(i, (i + k) % group_size) for i in range(group_size)])
        for k in range(1, group_size)
    ]
    owners = (sub - jnp.arange(group_size, dtype=jnp.int32)) % group_size
    pieces = jnp.take(jnp.stack(shifted), owners, axis=0)
    pieces = pieces.reshape(2, 2, BUFFER, 2, quarter).transpose(0, 2, 3, 1, 4)
    key_part = pieces[0].reshape(BUFFER, HD)
    value_part = pieces[1].reshape(BUFFER, HD)

    score_scale = 1.0 / math.sqrt(HD)
    key_pos = all_pos
    allowed = (segment[None, :] == query_seg[:, None]) & query_valid[:, None] & (
        key_pos[None, :] <= query_pos[:, None]
    ) | (key_pos[None, :] == query_pos[:, None])
    scores = (
        jnp.einsum("rhd,kd->rhk", queries, key_part, preferred_element_type=jnp.float32)
        * score_scale
    )
    scores = jnp.where(allowed[:, None, :], scores, MASK_FILL)
    new_max = jnp.max(scores, axis=2)
    prob_terms = jnp.where(allowed[:, None, :], jnp.exp(scores - new_max[:, :, None]), 0.0)
    totals = jnp.sum(prob_terms, axis=2)
    accum = jnp.einsum(
        "rhk,kd->rhd",
        prob_terms.astype(jnp.bfloat16),
        value_part,
        preferred_element_type=jnp.float32,
    )
    attended = (
        (accum / totals[:, :, None]).reshape(local_rows, head_count * HD).astype(jnp.bfloat16)
    )
    return jnp.where(query_valid[:, None], attended, jnp.zeros((), jnp.bfloat16))


def solution(mesh):
    heads_per_kv = QH // KVH
    tp_count = mesh.shape["tp"]
    group_size = heads_per_kv * tp_count // QH
    x_count = 4
    z_count = tp_count // x_count
    devices = mesh.devices.reshape(
        mesh.shape["rep"], mesh.shape["seq"], x_count, z_count // group_size, group_size
    )
    grid = jax.sharding.Mesh(devices, ("rep", "seq", "x", "zh", "zl"))
    tp = ("x", "zh", "zl")
    in_specs = (
        P("rep", ("seq",) + tp),
        P(),
        P("seq", tp),
        P(None, tp, None),
        P(),
        P(),
    )
    out_specs = P(("rep", "seq"), tp)
    return jax.shard_map(local, mesh=grid, in_specs=in_specs, out_specs=out_specs, check_vma=False)
```

```python
import math

import jax
import jax.numpy as jnp
from jax import lax
from jax.sharding import PartitionSpec as P

D = 8192
QH = 64
KVH = 8
HD = 128
RESP = 2
LMAX = 192
LMIN = 128
BUFFER = 384


ROPE_BASE = 500000.0
NORM_EPS = 1e-05
MASK_FILL = -1e30


def response_tables(lengths, routes):
    flat_len = lengths.reshape(-1)
    flat_route = routes.reshape(-1)
    response_ids = jnp.arange(flat_len.shape[0], dtype=jnp.int32)
    group_of = response_ids // RESP
    same_route = flat_route[:, None] == flat_route[None, :]
    same_group = group_of[:, None] == group_of[None, :]
    earlier = response_ids[None, :] < response_ids[:, None]
    dest_off = jnp.sum(jnp.where(same_route & earlier, flat_len[None, :], 0), axis=1)
    pair_off = jnp.sum(jnp.where(same_route & same_group & earlier, flat_len[None, :], 0), axis=1)
    src_start = jnp.sum(jnp.where(same_group & earlier, flat_len[None, :], 0), axis=1)
    return (flat_len, flat_route, group_of, dest_off, pair_off, src_start)


def locate(positions, replica, tables):
    flat_len, flat_route, group_of, dest_off, pair_off, src_start = tables
    response_ids = jnp.arange(flat_len.shape[0], dtype=jnp.int32)
    position_col = positions[:, None]
    inside = (
        (flat_route[None, :] == replica)
        & (dest_off[None, :] <= position_col)
        & (position_col < dest_off[None, :] + flat_len[None, :])
    )
    inside_int = inside.astype(jnp.int32)
    segment = jnp.sum(inside_int * (response_ids[None, :] + 1), axis=1) - 1
    seg_start = jnp.sum(inside_int * dest_off[None, :], axis=1)
    source_group = jnp.sum(inside_int * group_of[None, :], axis=1)
    pair_first = jnp.sum(inside_int * (dest_off - pair_off)[None, :], axis=1)
    source = jnp.sum(inside_int * src_start[None, :], axis=1)
    within = jnp.where(segment >= 0, positions - seg_start, 0)
    return (segment, within, source_group, pair_first, source)


def rotary(values_in, within):
    head_dim = values_in.shape[-1]
    half_dim = head_dim // 2
    freq_index = jnp.arange(half_dim, dtype=jnp.float32)
    inverse = jnp.power(ROPE_BASE, -2.0 * freq_index / head_dim)
    angles = within.astype(jnp.float32)[:, None] * inverse[None, :]
    cosine = jnp.cos(angles)[:, None, :]
    sine_part = jnp.sin(angles)[:, None, :]
    lower_half = values_in[..., :half_dim]
    upper_half = values_in[..., half_dim:]
    return jnp.concatenate(
        [
            lower_half * cosine - upper_half * sine_part,
            upper_half * cosine + lower_half * sine_part,
        ],
        axis=-1,
    )


def fill_rows(table, indices, present):
    taken = jnp.take(table, indices.reshape(-1), axis=0)
    return jnp.where(present.reshape(-1)[:, None], taken, jnp.zeros((), table.dtype))


def chunk_partials(rows, gain_grid, w_q, w_kv):
    rows_f = rows.astype(jnp.float32)
    scaled = (rows_f * gain_grid[:, :, None, :]).astype(jnp.bfloat16)
    squares = jnp.sum(rows_f * rows_f, axis=(0, 1, 3))
    query_part = jnp.einsum("zxri,xzic->rc", scaled, w_q, preferred_element_type=jnp.float32)
    kv_part = jnp.einsum("zxri,xzic->rc", scaled, w_kv, preferred_element_type=jnp.float32)
    return query_part, kv_part, squares


def local(hidden, gain, w_query, w_keyval, lengths, routes):
    rep_count = lax.axis_size("rep")
    seq_count = lax.axis_size("seq")
    x_count = lax.axis_size("x")
    group_size = lax.axis_size("zl")
    z_count = lax.axis_size("zh") * group_size
    tp_count = x_count * z_count
    replica = lax.axis_index("rep")
    seq_index = lax.axis_index("seq")
    partner = seq_count - 1 - seq_index
    sub = lax.axis_index("zl")
    feature_cols = hidden.shape[1]
    local_rows = BUFFER // seq_count
    window = BUFFER - LMIN
    rest = BUFFER - window
    head_count = w_query.shape[1] // HD
    query_cols = w_query.shape[1]
    kv_cols = 2 * HD // group_size
    quarter = HD // 4

    tables = response_tables(lengths, routes)
    flat_len, flat_route, group_of, dest_off, pair_off, src_start = tables
    my_route = lax.dynamic_slice_in_dim(flat_route, replica * RESP, RESP)
    my_start = lax.dynamic_slice_in_dim(src_start, replica * RESP, RESP)
    first_block = lax.dynamic_slice_in_dim(hidden, my_start[0], LMAX, 0)
    second_block = lax.dynamic_slice_in_dim(hidden, my_start[1], LMAX, 0)
    targets = jnp.arange(rep_count, dtype=jnp.int32)
    outgoing = jnp.where(
        (targets == my_route[0])[:, None, None], first_block[None], second_block[None]
    ).reshape(rep_count * LMAX, feature_cols)
    incoming = lax.all_to_all(outgoing, "rep", split_axis=0, concat_axis=0, tiled=True)
    all_pos = jnp.arange(BUFFER, dtype=jnp.int32)
    segment, within, source_group, pair_first, source = locate(all_pos, replica, tables)
    valid = segment >= 0
    gathered_idx = jnp.where(valid, source_group * LMAX + all_pos - pair_first, 0)
    assembled = fill_rows(incoming, gathered_idx, valid)

    w_half = lax.dynamic_index_in_dim(w_keyval, seq_index, 0, keepdims=False)
    w_half = w_half.reshape(feature_cols, KVH, 2, 2, 2, quarter)
    w_half = w_half.transpose(1, 2, 4, 0, 3, 5).reshape(tp_count, feature_cols, kv_cols)
    w_kv = lax.all_to_all(w_half, ("x", "zh", "zl"), split_axis=0, concat_axis=0, tiled=True)
    w_kv = w_kv.reshape(x_count, z_count, feature_cols, kv_cols)
    w_q = w_query.reshape(x_count, z_count, feature_cols, query_cols)
    gain_grid = lax.dynamic_index_in_dim(
        gain.reshape(seq_count, x_count, z_count, feature_cols), seq_index, 0, keepdims=False
    ).transpose(1, 0, 2)

    by_x = lax.all_gather(assembled, "x", axis=1, tiled=False)
    first_at = partner * rest
    second_at = seq_index * window
    first_rows = lax.dynamic_slice_in_dim(by_x, first_at, window, 0)
    second_rows = lax.dynamic_slice_in_dim(by_x, second_at, rest, 0)
    first_all = lax.all_gather(first_rows.transpose(1, 0, 2), ("zh", "zl"), axis=0, tiled=False)
    first_q, first_kv, first_sq = chunk_partials(first_all, gain_grid, w_q, w_kv)
    shift = partner * (local_rows - rest)
    payload = jnp.concatenate(
        [
            lax.dynamic_slice_in_dim(first_q, shift, local_rows, 0).reshape(-1),
            first_kv.reshape(-1),
            first_sq,
        ]
    )
    second_rows = second_rows.transpose(1, 0, 2)
    payload, second_rows = lax.optimization_barrier((payload, second_rows))
    got = lax.ppermute(payload, "seq", perm=[(0, 1), (1, 0)])
    second_all = lax.all_gather(second_rows, ("zh", "zl"), axis=0, tiled=False)
    got, second_all = lax.optimization_barrier((got, second_all))
    second_q, second_kv, second_sq = chunk_partials(second_all, gain_grid, w_q, w_kv)

    low_first = seq_index > 0
    own_q = jnp.where(
        low_first,
        jnp.concatenate([first_q, second_q], axis=0),
        jnp.concatenate([second_q, first_q], axis=0),
    )
    own_kv = jnp.where(
        low_first,
        jnp.concatenate([first_kv, second_kv], axis=0),
        jnp.concatenate([second_kv, first_kv], axis=0),
    )
    own_sq = jnp.where(
        low_first,
        jnp.concatenate([first_sq, second_sq], axis=0),
        jnp.concatenate([second_sq, first_sq], axis=0),
    )
    q_size = local_rows * query_cols
    kv_size = window * kv_cols
    got_query = got[:q_size].reshape(local_rows, query_cols)
    got_kv = got[q_size : q_size + kv_size].reshape(window, kv_cols)
    got_sq = got[q_size + kv_size :]

    win_at = seq_index * rest
    query_at = seq_index * local_rows
    query_raw = lax.dynamic_slice_in_dim(own_q, query_at, local_rows, 0) + got_query
    kv_raw = lax.dynamic_slice_in_dim(own_kv, win_at, window, 0) + got_kv
    win_rms = lax.rsqrt((lax.dynamic_slice_in_dim(own_sq, win_at, window) + got_sq) / D + NORM_EPS)
    query_rms = lax.dynamic_slice_in_dim(win_rms, query_at - win_at, local_rows)

    query_pos = query_at + jnp.arange(local_rows, dtype=jnp.int32)
    query_seg = lax.dynamic_slice_in_dim(segment, query_at, local_rows)
    query_within = lax.dynamic_slice_in_dim(within, query_at, local_rows)
    query_valid = query_seg >= 0
    queries = rotary(
        query_rms[:, None, None] * query_raw.reshape(local_rows, head_count, HD), query_within
    ).astype(jnp.bfloat16)

    key_pos = win_at + jnp.arange(window, dtype=jnp.int32)
    key_seg = lax.dynamic_slice_in_dim(segment, win_at, window)
    key_within = lax.dynamic_slice_in_dim(within, win_at, window)
    kv_scaled = (win_rms[:, None] * kv_raw).reshape(window, 2, quarter)
    freq_index = (sub % 2 * quarter + jnp.arange(quarter, dtype=jnp.int32)).astype(jnp.float32)
    inverse = jnp.power(ROPE_BASE, -2.0 * freq_index / HD)
    angles = key_within.astype(jnp.float32)[:, None] * inverse[None, :]
    cosine = jnp.cos(angles)
    sine_part = jnp.sin(angles)
    lower_half = kv_scaled[:, 0]
    upper_half = kv_scaled[:, 1]
    roped = jnp.stack(
        [lower_half * cosine - upper_half * sine_part, upper_half * cosine + lower_half * sine_part],
        axis=1,
    )
    piece = jnp.where(sub < 2, roped, kv_scaled).astype(jnp.bfloat16)
    shifted = [piece] + [
        lax.ppermute(piece, "zl", perm=[(i, (i + k) % group_size) for i in range(group_size)])
        for k in range(1, group_size)
    ]
    owners = (sub - jnp.arange(group_size, dtype=jnp.int32)) % group_size
    pieces = jnp.take(jnp.stack(shifted), owners, axis=0)
    pieces = pieces.reshape(2, 2, window, 2, quarter).transpose(0, 2, 3, 1, 4)
    key_part = pieces[0].reshape(window, HD)
    value_part = pieces[1].reshape(window, HD)

    score_scale = 1.0 / math.sqrt(HD)
    allowed = (key_seg[None, :] == query_seg[:, None]) & query_valid[:, None] & (
        key_pos[None, :] <= query_pos[:, None]
    ) | (key_pos[None, :] == query_pos[:, None])
    scores = (
        jnp.einsum("rhd,kd->rhk", queries, key_part, preferred_element_type=jnp.float32)
        * score_scale
    )
    scores = jnp.where(allowed[:, None, :], scores, MASK_FILL)
    new_max = jnp.max(scores, axis=2)
    prob_terms = jnp.where(allowed[:, None, :], jnp.exp(scores - new_max[:, :, None]), 0.0)
    totals = jnp.sum(prob_terms, axis=2)
    accum = jnp.einsum(
        "rhk,kd->rhd",
        prob_terms.astype(jnp.bfloat16),
        value_part,
        preferred_element_type=jnp.float32,
    )
    attended = (
        (accum / totals[:, :, None]).reshape(local_rows, head_count * HD).astype(jnp.bfloat16)
    )
    return jnp.where(query_valid[:, None], attended, jnp.zeros((), jnp.bfloat16))


def solution(mesh):
    heads_per_kv = QH // KVH
    tp_count = mesh.shape["tp"]
    group_size = heads_per_kv * tp_count // QH
    x_count = 4
    z_count = tp_count // x_count
    devices = mesh.devices.reshape(
        mesh.shape["rep"], mesh.shape["seq"], x_count, z_count // group_size, group_size
    )
    grid = jax.sharding.Mesh(devices, ("rep", "seq", "x", "zh", "zl"))
    tp = ("x", "zh", "zl")
    in_specs = (
        P("rep", ("seq",) + tp),
        P(),
        P("seq", tp),
        P(None, tp, None),
        P(),
        P(),
    )
    out_specs = P(("rep", "seq"), tp)
    return jax.shard_map(local, mesh=grid, in_specs=in_specs, out_specs=out_specs, check_vma=False)
```

```python
import math

import jax
import jax.numpy as jnp
from jax import lax
from jax.sharding import PartitionSpec as P

D = 8192
QH = 64
KVH = 8
HD = 128
RESP = 2
LMAX = 192
LMIN = 128
BUFFER = 384


ROPE_BASE = 500000.0
NORM_EPS = 1e-05
MASK_FILL = -1e30


def response_tables(lengths, routes):
    flat_len = lengths.reshape(-1)
    flat_route = routes.reshape(-1)
    response_ids = jnp.arange(flat_len.shape[0], dtype=jnp.int32)
    group_of = response_ids // RESP
    same_route = flat_route[:, None] == flat_route[None, :]
    same_group = group_of[:, None] == group_of[None, :]
    earlier = response_ids[None, :] < response_ids[:, None]
    dest_off = jnp.sum(jnp.where(same_route & earlier, flat_len[None, :], 0), axis=1)
    pair_off = jnp.sum(jnp.where(same_route & same_group & earlier, flat_len[None, :], 0), axis=1)
    src_start = jnp.sum(jnp.where(same_group & earlier, flat_len[None, :], 0), axis=1)
    return (flat_len, flat_route, group_of, dest_off, pair_off, src_start)


def locate(positions, replica, tables):
    flat_len, flat_route, group_of, dest_off, pair_off, src_start = tables
    response_ids = jnp.arange(flat_len.shape[0], dtype=jnp.int32)
    position_col = positions[:, None]
    inside = (
        (flat_route[None, :] == replica)
        & (dest_off[None, :] <= position_col)
        & (position_col < dest_off[None, :] + flat_len[None, :])
    )
    inside_int = inside.astype(jnp.int32)
    segment = jnp.sum(inside_int * (response_ids[None, :] + 1), axis=1) - 1
    seg_start = jnp.sum(inside_int * dest_off[None, :], axis=1)
    source_group = jnp.sum(inside_int * group_of[None, :], axis=1)
    pair_first = jnp.sum(inside_int * (dest_off - pair_off)[None, :], axis=1)
    source = jnp.sum(inside_int * src_start[None, :], axis=1)
    within = jnp.where(segment >= 0, positions - seg_start, 0)
    return (segment, within, source_group, pair_first, source)


def rotary(values_in, within):
    head_dim = values_in.shape[-1]
    half_dim = head_dim // 2
    freq_index = jnp.arange(half_dim, dtype=jnp.float32)
    inverse = jnp.power(ROPE_BASE, -2.0 * freq_index / head_dim)
    angles = within.astype(jnp.float32)[:, None] * inverse[None, :]
    cosine = jnp.cos(angles)[:, None, :]
    sine_part = jnp.sin(angles)[:, None, :]
    lower_half = values_in[..., :half_dim]
    upper_half = values_in[..., half_dim:]
    return jnp.concatenate(
        [
            lower_half * cosine - upper_half * sine_part,
            upper_half * cosine + lower_half * sine_part,
        ],
        axis=-1,
    )


def fill_rows(table, indices, present):
    taken = jnp.take(table, indices.reshape(-1), axis=0)
    return jnp.where(present.reshape(-1)[:, None], taken, jnp.zeros((), table.dtype))


def local(hidden, gain, w_query, w_keyval, lengths, routes):
    rep_count = lax.axis_size("rep")
    seq_count = lax.axis_size("seq")
    x_count = lax.axis_size("x")
    group_size = lax.axis_size("zl")
    z_count = lax.axis_size("zh") * group_size
    tp_count = x_count * z_count
    replica = lax.axis_index("rep")
    seq_index = lax.axis_index("seq")
    sub = lax.axis_index("zl")
    feature_cols = hidden.shape[1]
    local_rows = BUFFER // seq_count
    head_count = w_query.shape[1] // HD
    kv_cols = 2 * HD // group_size
    quarter = HD // 4

    tables = response_tables(lengths, routes)
    flat_len, flat_route, group_of, dest_off, pair_off, src_start = tables
    my_route = lax.dynamic_slice_in_dim(flat_route, replica * RESP, RESP)
    my_start = lax.dynamic_slice_in_dim(src_start, replica * RESP, RESP)
    first_block = lax.dynamic_slice_in_dim(hidden, my_start[0], LMAX, 0)
    second_block = lax.dynamic_slice_in_dim(hidden, my_start[1], LMAX, 0)
    targets = jnp.arange(rep_count, dtype=jnp.int32)
    outgoing = jnp.where(
        (targets == my_route[0])[:, None, None], first_block[None], second_block[None]
    ).reshape(rep_count * LMAX, feature_cols)
    w_half = lax.dynamic_index_in_dim(w_keyval, seq_index, 0, keepdims=False)
    w_half = w_half.reshape(feature_cols, KVH, 2, 2, 2, quarter)
    w_half = w_half.transpose(1, 2, 4, 0, 3, 5).reshape(tp_count, feature_cols, kv_cols)
    w_kv = lax.all_to_all(w_half, ("x", "zh", "zl"), split_axis=0, concat_axis=0, tiled=True)
    incoming = lax.all_to_all(outgoing, "rep", split_axis=0, concat_axis=0, tiled=True)
    w_kv, incoming = lax.optimization_barrier((w_kv, incoming))
    w_kv = w_kv.reshape(x_count, z_count, feature_cols, kv_cols)
    all_pos = jnp.arange(BUFFER, dtype=jnp.int32)
    segment, within, source_group, pair_first, source = locate(all_pos, replica, tables)
    valid = segment >= 0
    gathered_idx = jnp.where(valid, source_group * LMAX + all_pos - pair_first, 0)
    assembled = fill_rows(incoming, gathered_idx, valid)

    gathered = lax.all_gather(assembled, "x", axis=0, tiled=False)
    gathered = lax.all_gather(gathered, ("zh", "zl"), axis=0, tiled=False)
    gain_half = lax.dynamic_index_in_dim(
        gain.reshape(seq_count, x_count, z_count, feature_cols), seq_index, 0, keepdims=False
    )
    gathered_f = gathered.astype(jnp.float32)
    scaled = (gathered_f * gain_half.transpose(1, 0, 2)[:, :, None, :]).astype(jnp.bfloat16)
    squares = jnp.sum(gathered_f * gathered_f, axis=(0, 1, 3))
    w_q = w_query.reshape(x_count, z_count, feature_cols, w_query.shape[1])
    query_part = jnp.einsum("zxri,xzic->rc", scaled, w_q, preferred_element_type=jnp.float32)
    kv_part = jnp.einsum("zxri,xzic->rc", scaled, w_kv, preferred_element_type=jnp.float32)

    window = BUFFER - LMIN
    rest = BUFFER - window
    partner = seq_count - 1 - seq_index
    query_cols = query_part.shape[1]
    payload = jnp.concatenate(
        [
            lax.dynamic_slice_in_dim(query_part, partner * local_rows, local_rows, 0).reshape(-1),
            lax.dynamic_slice_in_dim(kv_part, partner * rest, window, 0).reshape(-1),
            lax.dynamic_slice_in_dim(squares, partner * rest, window),
        ]
    )
    got = lax.ppermute(payload, "seq", perm=[(0, 1), (1, 0)])
    q_size = local_rows * query_cols
    kv_size = window * kv_cols
    win_at = seq_index * rest
    query_at = seq_index * local_rows
    query_raw = lax.dynamic_slice_in_dim(query_part, query_at, local_rows, 0) + got[
        :q_size
    ].reshape(local_rows, query_cols)
    kv_raw = lax.dynamic_slice_in_dim(kv_part, win_at, window, 0) + got[
        q_size : q_size + kv_size
    ].reshape(window, kv_cols)
    win_squares = lax.dynamic_slice_in_dim(squares, win_at, window) + got[q_size + kv_size :]
    win_rms = lax.rsqrt(win_squares / D + NORM_EPS)
    query_rms = lax.dynamic_slice_in_dim(win_rms, query_at - win_at, local_rows)

    query_pos = query_at + jnp.arange(local_rows, dtype=jnp.int32)
    query_seg = lax.dynamic_slice_in_dim(segment, query_at, local_rows)
    query_within = lax.dynamic_slice_in_dim(within, query_at, local_rows)
    query_valid = query_seg >= 0
    queries = rotary(
        query_rms[:, None, None] * query_raw.reshape(local_rows, head_count, HD), query_within
    ).astype(jnp.bfloat16)

    key_pos = win_at + jnp.arange(window, dtype=jnp.int32)
    key_seg = lax.dynamic_slice_in_dim(segment, win_at, window)
    key_within = lax.dynamic_slice_in_dim(within, win_at, window)
    kv_scaled = (win_rms[:, None] * kv_raw).reshape(window, 2, quarter)
    freq_index = (sub % 2 * quarter + jnp.arange(quarter, dtype=jnp.int32)).astype(jnp.float32)
    inverse = jnp.power(ROPE_BASE, -2.0 * freq_index / HD)
    angles = key_within.astype(jnp.float32)[:, None] * inverse[None, :]
    cosine = jnp.cos(angles)
    sine_part = jnp.sin(angles)
    lower_half = kv_scaled[:, 0]
    upper_half = kv_scaled[:, 1]
    roped = jnp.stack(
        [lower_half * cosine - upper_half * sine_part, upper_half * cosine + lower_half * sine_part],
        axis=1,
    )
    piece = jnp.where(sub < 2, roped, kv_scaled).astype(jnp.bfloat16)
    spread = jnp.broadcast_to(piece[None], (group_size,) + piece.shape)
    pieces = lax.all_to_all(spread, "zl", split_axis=0, concat_axis=0, tiled=True)
    pieces = pieces.reshape(2, 2, window, 2, quarter).transpose(0, 2, 3, 1, 4)
    key_part = pieces[0].reshape(window, HD)
    value_part = pieces[1].reshape(window, HD)

    score_scale = 1.0 / math.sqrt(HD)
    allowed = (key_seg[None, :] == query_seg[:, None]) & query_valid[:, None] & (
        key_pos[None, :] <= query_pos[:, None]
    ) | (key_pos[None, :] == query_pos[:, None])
    scores = (
        jnp.einsum("rhd,kd->rhk", queries, key_part, preferred_element_type=jnp.float32)
        * score_scale
    )
    scores = jnp.where(allowed[:, None, :], scores, MASK_FILL)
    new_max = jnp.max(scores, axis=2)
    prob_terms = jnp.where(allowed[:, None, :], jnp.exp(scores - new_max[:, :, None]), 0.0)
    totals = jnp.sum(prob_terms, axis=2)
    accum = jnp.einsum(
        "rhk,kd->rhd",
        prob_terms.astype(jnp.bfloat16),
        value_part,
        preferred_element_type=jnp.float32,
    )
    attended = (
        (accum / totals[:, :, None]).reshape(local_rows, head_count * HD).astype(jnp.bfloat16)
    )
    return jnp.where(query_valid[:, None], attended, jnp.zeros((), jnp.bfloat16))


def solution(mesh):
    heads_per_kv = QH // KVH
    tp_count = mesh.shape["tp"]
    group_size = heads_per_kv * tp_count // QH
    x_count = 4
    z_count = tp_count // x_count
    devices = mesh.devices.reshape(
        mesh.shape["rep"], mesh.shape["seq"], x_count, z_count // group_size, group_size
    )
    grid = jax.sharding.Mesh(devices, ("rep", "seq", "x", "zh", "zl"))
    tp = ("x", "zh", "zl")
    in_specs = (
        P("rep", ("seq",) + tp),
        P(),
        P("seq", tp),
        P(None, tp, None),
        P(),
        P(),
    )
    out_specs = P(("rep", "seq"), tp)
    return jax.shard_map(local, mesh=grid, in_specs=in_specs, out_specs=out_specs, check_vma=False)
```

```python
import math

import jax
import jax.numpy as jnp
from jax import lax
from jax.sharding import PartitionSpec as P

D = 8192
QH = 64
KVH = 8
HD = 128
RESP = 2
LMAX = 192
LMIN = 128
BUFFER = 384


ROPE_BASE = 500000.0
NORM_EPS = 1e-05
MASK_FILL = -1e30


def response_tables(lengths, routes):
    flat_len = lengths.reshape(-1)
    flat_route = routes.reshape(-1)
    response_ids = jnp.arange(flat_len.shape[0], dtype=jnp.int32)
    group_of = response_ids // RESP
    same_route = flat_route[:, None] == flat_route[None, :]
    same_group = group_of[:, None] == group_of[None, :]
    earlier = response_ids[None, :] < response_ids[:, None]
    dest_off = jnp.sum(jnp.where(same_route & earlier, flat_len[None, :], 0), axis=1)
    pair_off = jnp.sum(jnp.where(same_route & same_group & earlier, flat_len[None, :], 0), axis=1)
    src_start = jnp.sum(jnp.where(same_group & earlier, flat_len[None, :], 0), axis=1)
    return (flat_len, flat_route, group_of, dest_off, pair_off, src_start)


def locate(positions, replica, tables):
    flat_len, flat_route, group_of, dest_off, pair_off, src_start = tables
    response_ids = jnp.arange(flat_len.shape[0], dtype=jnp.int32)
    position_col = positions[:, None]
    inside = (
        (flat_route[None, :] == replica)
        & (dest_off[None, :] <= position_col)
        & (position_col < dest_off[None, :] + flat_len[None, :])
    )
    inside_int = inside.astype(jnp.int32)
    segment = jnp.sum(inside_int * (response_ids[None, :] + 1), axis=1) - 1
    seg_start = jnp.sum(inside_int * dest_off[None, :], axis=1)
    source_group = jnp.sum(inside_int * group_of[None, :], axis=1)
    pair_first = jnp.sum(inside_int * (dest_off - pair_off)[None, :], axis=1)
    source = jnp.sum(inside_int * src_start[None, :], axis=1)
    within = jnp.where(segment >= 0, positions - seg_start, 0)
    return (segment, within, source_group, pair_first, source)


def rotary(values_in, within):
    head_dim = values_in.shape[-1]
    half_dim = head_dim // 2
    freq_index = jnp.arange(half_dim, dtype=jnp.float32)
    inverse = jnp.power(ROPE_BASE, -2.0 * freq_index / head_dim)
    angles = within.astype(jnp.float32)[:, None] * inverse[None, :]
    cosine = jnp.cos(angles)[:, None, :]
    sine_part = jnp.sin(angles)[:, None, :]
    lower_half = values_in[..., :half_dim]
    upper_half = values_in[..., half_dim:]
    return jnp.concatenate(
        [
            lower_half * cosine - upper_half * sine_part,
            upper_half * cosine + lower_half * sine_part,
        ],
        axis=-1,
    )


def fill_rows(table, indices, present):
    taken = jnp.take(table, indices.reshape(-1), axis=0)
    return jnp.where(present.reshape(-1)[:, None], taken, jnp.zeros((), table.dtype))


def local(hidden, gain, w_query, w_keyval, lengths, routes):
    rep_count = lax.axis_size("rep")
    seq_count = lax.axis_size("seq")
    x_count = lax.axis_size("x")
    group_size = lax.axis_size("zl")
    z_count = lax.axis_size("zh") * group_size
    tp_count = x_count * z_count
    replica = lax.axis_index("rep")
    seq_index = lax.axis_index("seq")
    sub = lax.axis_index("zl")
    feature_cols = hidden.shape[1]
    local_rows = BUFFER // seq_count
    head_count = w_query.shape[1] // HD
    kv_cols = 2 * HD // group_size
    quarter = HD // 4

    tables = response_tables(lengths, routes)
    flat_len, flat_route, group_of, dest_off, pair_off, src_start = tables
    my_route = lax.dynamic_slice_in_dim(flat_route, replica * RESP, RESP)
    my_start = lax.dynamic_slice_in_dim(src_start, replica * RESP, RESP)
    first_block = lax.dynamic_slice_in_dim(hidden, my_start[0], LMAX, 0)
    second_block = lax.dynamic_slice_in_dim(hidden, my_start[1], LMAX, 0)
    targets = jnp.arange(rep_count, dtype=jnp.int32)
    outgoing = jnp.where(
        (targets == my_route[0])[:, None, None], first_block[None], second_block[None]
    ).reshape(rep_count * LMAX, feature_cols)
    w_half = lax.dynamic_index_in_dim(w_keyval, seq_index, 0, keepdims=False)
    w_half = w_half.reshape(feature_cols, KVH, 2, 2, 2, quarter)
    w_half = w_half.transpose(1, 2, 4, 0, 3, 5).reshape(tp_count, feature_cols, kv_cols)
    w_kv = lax.all_to_all(w_half, ("x", "zh", "zl"), split_axis=0, concat_axis=0, tiled=True)
    incoming = lax.all_to_all(outgoing, "rep", split_axis=0, concat_axis=0, tiled=True)
    w_kv = w_kv.reshape(x_count, z_count, feature_cols, kv_cols)
    all_pos = jnp.arange(BUFFER, dtype=jnp.int32)
    segment, within, source_group, pair_first, source = locate(all_pos, replica, tables)
    valid = segment >= 0
    gathered_idx = jnp.where(valid, source_group * LMAX + all_pos - pair_first, 0)
    assembled = fill_rows(incoming, gathered_idx, valid)

    gathered = lax.all_gather(assembled, "x", axis=0, tiled=False)
    gathered = lax.all_gather(gathered, ("zh", "zl"), axis=0, tiled=False)
    gain_half = lax.dynamic_index_in_dim(
        gain.reshape(seq_count, x_count, z_count, feature_cols), seq_index, 0, keepdims=False
    )
    gathered_f = gathered.astype(jnp.float32)
    scaled = (gathered_f * gain_half.transpose(1, 0, 2)[:, :, None, :]).astype(jnp.bfloat16)
    squares = jnp.sum(gathered_f * gathered_f, axis=(0, 1, 3))
    w_q = w_query.reshape(x_count, z_count, feature_cols, w_query.shape[1])
    query_part = jnp.einsum("zxri,xzic->rc", scaled, w_q, preferred_element_type=jnp.float32)
    kv_part = jnp.einsum("zxri,xzic->rc", scaled, w_kv, preferred_element_type=jnp.float32)

    window = BUFFER - LMIN
    rest = BUFFER - window
    partner = seq_count - 1 - seq_index
    query_cols = query_part.shape[1]
    payload = jnp.concatenate(
        [
            lax.dynamic_slice_in_dim(query_part, partner * local_rows, local_rows, 0).reshape(-1),
            lax.dynamic_slice_in_dim(kv_part, partner * rest, window, 0).reshape(-1),
            lax.dynamic_slice_in_dim(squares, partner * rest, window),
        ]
    )
    got = lax.ppermute(payload, "seq", perm=[(0, 1), (1, 0)])
    q_size = local_rows * query_cols
    kv_size = window * kv_cols
    win_at = seq_index * rest
    query_at = seq_index * local_rows
    query_raw = lax.dynamic_slice_in_dim(query_part, query_at, local_rows, 0) + got[
        :q_size
    ].reshape(local_rows, query_cols)
    kv_raw = lax.dynamic_slice_in_dim(kv_part, win_at, window, 0) + got[
        q_size : q_size + kv_size
    ].reshape(window, kv_cols)
    win_squares = lax.dynamic_slice_in_dim(squares, win_at, window) + got[q_size + kv_size :]
    win_rms = lax.rsqrt(win_squares / D + NORM_EPS)
    query_rms = lax.dynamic_slice_in_dim(win_rms, query_at - win_at, local_rows)

    query_pos = query_at + jnp.arange(local_rows, dtype=jnp.int32)
    query_seg = lax.dynamic_slice_in_dim(segment, query_at, local_rows)
    query_within = lax.dynamic_slice_in_dim(within, query_at, local_rows)
    query_valid = query_seg >= 0
    queries = rotary(
        query_rms[:, None, None] * query_raw.reshape(local_rows, head_count, HD), query_within
    ).astype(jnp.bfloat16)

    key_pos = win_at + jnp.arange(window, dtype=jnp.int32)
    key_seg = lax.dynamic_slice_in_dim(segment, win_at, window)
    key_within = lax.dynamic_slice_in_dim(within, win_at, window)
    kv_scaled = (win_rms[:, None] * kv_raw).reshape(window, 2, quarter)
    freq_index = (sub % 2 * quarter + jnp.arange(quarter, dtype=jnp.int32)).astype(jnp.float32)
    inverse = jnp.power(ROPE_BASE, -2.0 * freq_index / HD)
    angles = key_within.astype(jnp.float32)[:, None] * inverse[None, :]
    cosine = jnp.cos(angles)
    sine_part = jnp.sin(angles)
    lower_half = kv_scaled[:, 0]
    upper_half = kv_scaled[:, 1]
    roped = jnp.stack(
        [lower_half * cosine - upper_half * sine_part, upper_half * cosine + lower_half * sine_part],
        axis=1,
    )
    piece = jnp.where(sub < 2, roped, kv_scaled).astype(jnp.bfloat16)
    spread = jnp.broadcast_to(piece[None], (group_size,) + piece.shape)
    pieces = lax.all_to_all(spread, "zl", split_axis=0, concat_axis=0, tiled=True)
    pieces = pieces.reshape(2, 2, window, 2, quarter).transpose(0, 2, 3, 1, 4)
    key_part = pieces[0].reshape(window, HD)
    value_part = pieces[1].reshape(window, HD)

    score_scale = 1.0 / math.sqrt(HD)
    allowed = (key_seg[None, :] == query_seg[:, None]) & query_valid[:, None] & (
        key_pos[None, :] <= query_pos[:, None]
    ) | (key_pos[None, :] == query_pos[:, None])
    scores = (
        jnp.einsum("rhd,kd->rhk", queries, key_part, preferred_element_type=jnp.float32)
        * score_scale
    )
    scores = jnp.where(allowed[:, None, :], scores, MASK_FILL)
    new_max = jnp.max(scores, axis=2)
    prob_terms = jnp.where(allowed[:, None, :], jnp.exp(scores - new_max[:, :, None]), 0.0)
    totals = jnp.sum(prob_terms, axis=2)
    accum = jnp.einsum(
        "rhk,kd->rhd",
        prob_terms.astype(jnp.bfloat16),
        value_part,
        preferred_element_type=jnp.float32,
    )
    attended = (
        (accum / totals[:, :, None]).reshape(local_rows, head_count * HD).astype(jnp.bfloat16)
    )
    return jnp.where(query_valid[:, None], attended, jnp.zeros((), jnp.bfloat16))


def solution(mesh):
    heads_per_kv = QH // KVH
    tp_count = mesh.shape["tp"]
    group_size = heads_per_kv * tp_count // QH
    x_count = 4
    z_count = tp_count // x_count
    devices = mesh.devices.reshape(
        mesh.shape["rep"], mesh.shape["seq"], x_count, z_count // group_size, group_size
    )
    grid = jax.sharding.Mesh(devices, ("rep", "seq", "x", "zh", "zl"))
    tp = ("x", "zh", "zl")
    in_specs = (
        P("rep", ("seq",) + tp),
        P(),
        P("seq", tp),
        P(None, tp, None),
        P(),
        P(),
    )
    out_specs = P(("rep", "seq"), tp)
    return jax.shard_map(local, mesh=grid, in_specs=in_specs, out_specs=out_specs, check_vma=False)
```

```python
import math

import jax
import jax.numpy as jnp
from jax import lax
from jax.sharding import PartitionSpec as P

D = 8192
QH = 64
KVH = 8
HD = 128
RESP = 2
LMAX = 192
LMIN = 128
BUFFER = 384


ROPE_BASE = 500000.0
NORM_EPS = 1e-05
MASK_FILL = -1e30


def response_tables(lengths, routes):
    flat_len = lengths.reshape(-1)
    flat_route = routes.reshape(-1)
    response_ids = jnp.arange(flat_len.shape[0], dtype=jnp.int32)
    group_of = response_ids // RESP
    same_route = flat_route[:, None] == flat_route[None, :]
    same_group = group_of[:, None] == group_of[None, :]
    earlier = response_ids[None, :] < response_ids[:, None]
    dest_off = jnp.sum(jnp.where(same_route & earlier, flat_len[None, :], 0), axis=1)
    pair_off = jnp.sum(jnp.where(same_route & same_group & earlier, flat_len[None, :], 0), axis=1)
    src_start = jnp.sum(jnp.where(same_group & earlier, flat_len[None, :], 0), axis=1)
    return (flat_len, flat_route, group_of, dest_off, pair_off, src_start)


def locate(positions, replica, tables):
    flat_len, flat_route, group_of, dest_off, pair_off, src_start = tables
    response_ids = jnp.arange(flat_len.shape[0], dtype=jnp.int32)
    position_col = positions[:, None]
    inside = (
        (flat_route[None, :] == replica)
        & (dest_off[None, :] <= position_col)
        & (position_col < dest_off[None, :] + flat_len[None, :])
    )
    inside_int = inside.astype(jnp.int32)
    segment = jnp.sum(inside_int * (response_ids[None, :] + 1), axis=1) - 1
    seg_start = jnp.sum(inside_int * dest_off[None, :], axis=1)
    source_group = jnp.sum(inside_int * group_of[None, :], axis=1)
    pair_first = jnp.sum(inside_int * (dest_off - pair_off)[None, :], axis=1)
    source = jnp.sum(inside_int * src_start[None, :], axis=1)
    within = jnp.where(segment >= 0, positions - seg_start, 0)
    return (segment, within, source_group, pair_first, source)


def rotary(values_in, within):
    head_dim = values_in.shape[-1]
    half_dim = head_dim // 2
    freq_index = jnp.arange(half_dim, dtype=jnp.float32)
    inverse = jnp.power(ROPE_BASE, -2.0 * freq_index / head_dim)
    angles = within.astype(jnp.float32)[:, None] * inverse[None, :]
    cosine = jnp.cos(angles)[:, None, :]
    sine_part = jnp.sin(angles)[:, None, :]
    lower_half = values_in[..., :half_dim]
    upper_half = values_in[..., half_dim:]
    return jnp.concatenate(
        [
            lower_half * cosine - upper_half * sine_part,
            upper_half * cosine + lower_half * sine_part,
        ],
        axis=-1,
    )


def fill_rows(table, indices, present):
    taken = jnp.take(table, indices.reshape(-1), axis=0)
    return jnp.where(present.reshape(-1)[:, None], taken, jnp.zeros((), table.dtype))


def local(hidden, gain, w_query, w_keyval, lengths, routes):
    rep_count = lax.axis_size("rep")
    seq_count = lax.axis_size("seq")
    x_count = lax.axis_size("x")
    group_size = lax.axis_size("zl")
    z_count = lax.axis_size("zh") * group_size
    tp_count = x_count * z_count
    replica = lax.axis_index("rep")
    seq_index = lax.axis_index("seq")
    sub = lax.axis_index("zl")
    feature_cols = hidden.shape[1]
    local_rows = BUFFER // seq_count
    head_count = w_query.shape[1] // HD
    kv_cols = 2 * HD // group_size
    quarter = HD // 4

    my_lengths = lax.dynamic_index_in_dim(lengths, replica, 0, keepdims=False)
    my_routes = lax.dynamic_index_in_dim(routes, replica, 0, keepdims=False)
    first_block = hidden[:LMAX]
    second_block = lax.dynamic_slice_in_dim(hidden, my_lengths[0], LMAX, 0)
    targets = jnp.arange(rep_count, dtype=jnp.int32)
    outgoing = jnp.where(
        (targets == my_routes[0])[:, None, None], first_block[None], second_block[None]
    ).reshape(rep_count * LMAX, feature_cols)
    w_half = lax.dynamic_index_in_dim(w_keyval, seq_index, 0, keepdims=False)
    w_half = w_half.reshape(feature_cols, KVH, 2, 2, 2, quarter)
    w_half = w_half.transpose(1, 2, 4, 0, 3, 5).reshape(tp_count, feature_cols, kv_cols)
    w_kv = lax.all_to_all(w_half, ("x", "zh", "zl"), split_axis=0, concat_axis=0, tiled=True)
    incoming = lax.all_to_all(outgoing, "rep", split_axis=0, concat_axis=0, tiled=True)
    w_kv = w_kv.reshape(x_count, z_count, feature_cols, kv_cols)
    tables = response_tables(lengths, routes)
    all_pos = jnp.arange(BUFFER, dtype=jnp.int32)
    segment, within, source_group, pair_first, source = locate(all_pos, replica, tables)
    valid = segment >= 0
    gathered_idx = jnp.where(valid, source_group * LMAX + all_pos - pair_first, 0)
    assembled = fill_rows(incoming, gathered_idx, valid)

    spread = jnp.broadcast_to(assembled[None], (x_count,) + assembled.shape)
    gathered = lax.all_to_all(spread, "x", split_axis=0, concat_axis=0, tiled=True)
    gathered = lax.all_gather(gathered, ("zh", "zl"), axis=0, tiled=False)
    gain_half = lax.dynamic_index_in_dim(
        gain.reshape(seq_count, x_count, z_count, feature_cols), seq_index, 0, keepdims=False
    )
    gathered_f = gathered.astype(jnp.float32)
    scaled = (gathered_f * gain_half.transpose(1, 0, 2)[:, :, None, :]).astype(jnp.bfloat16)
    squares = jnp.sum(gathered_f * gathered_f, axis=(0, 1, 3))
    w_q = w_query.reshape(x_count, z_count, feature_cols, w_query.shape[1])
    query_part = jnp.einsum("zxri,xzic->rc", scaled, w_q, preferred_element_type=jnp.float32)
    kv_part = jnp.einsum("zxri,xzic->rc", scaled, w_kv, preferred_element_type=jnp.float32)

    window = BUFFER - LMIN
    rest = BUFFER - window
    partner = seq_count - 1 - seq_index
    query_cols = query_part.shape[1]
    payload = jnp.concatenate(
        [
            lax.dynamic_slice_in_dim(query_part, partner * local_rows, local_rows, 0).reshape(-1),
            lax.dynamic_slice_in_dim(kv_part, partner * rest, window, 0).reshape(-1),
            lax.dynamic_slice_in_dim(squares, partner * rest, window),
        ]
    )
    got = lax.ppermute(payload, "seq", perm=[(0, 1), (1, 0)])
    q_size = local_rows * query_cols
    kv_size = window * kv_cols
    win_at = seq_index * rest
    query_at = seq_index * local_rows
    query_raw = lax.dynamic_slice_in_dim(query_part, query_at, local_rows, 0) + got[
        :q_size
    ].reshape(local_rows, query_cols)
    kv_raw = lax.dynamic_slice_in_dim(kv_part, win_at, window, 0) + got[
        q_size : q_size + kv_size
    ].reshape(window, kv_cols)
    win_squares = lax.dynamic_slice_in_dim(squares, win_at, window) + got[q_size + kv_size :]
    win_rms = lax.rsqrt(win_squares / D + NORM_EPS)
    query_rms = lax.dynamic_slice_in_dim(win_rms, query_at - win_at, local_rows)

    query_pos = query_at + jnp.arange(local_rows, dtype=jnp.int32)
    query_seg = lax.dynamic_slice_in_dim(segment, query_at, local_rows)
    query_within = lax.dynamic_slice_in_dim(within, query_at, local_rows)
    query_valid = query_seg >= 0
    queries = rotary(
        query_rms[:, None, None] * query_raw.reshape(local_rows, head_count, HD), query_within
    ).astype(jnp.bfloat16)

    key_pos = win_at + jnp.arange(window, dtype=jnp.int32)
    key_seg = lax.dynamic_slice_in_dim(segment, win_at, window)
    key_within = lax.dynamic_slice_in_dim(within, win_at, window)
    kv_scaled = (win_rms[:, None] * kv_raw).reshape(window, 2, quarter)
    freq_index = (sub % 2 * quarter + jnp.arange(quarter, dtype=jnp.int32)).astype(jnp.float32)
    inverse = jnp.power(ROPE_BASE, -2.0 * freq_index / HD)
    angles = key_within.astype(jnp.float32)[:, None] * inverse[None, :]
    cosine = jnp.cos(angles)
    sine_part = jnp.sin(angles)
    lower_half = kv_scaled[:, 0]
    upper_half = kv_scaled[:, 1]
    roped = jnp.stack(
        [lower_half * cosine - upper_half * sine_part, upper_half * cosine + lower_half * sine_part],
        axis=1,
    )
    piece = jnp.where(sub < 2, roped, kv_scaled).astype(jnp.bfloat16)
    spread = jnp.broadcast_to(piece[None], (group_size,) + piece.shape)
    pieces = lax.all_to_all(spread, "zl", split_axis=0, concat_axis=0, tiled=True)
    pieces = pieces.reshape(2, 2, window, 2, quarter).transpose(0, 2, 3, 1, 4)
    key_part = pieces[0].reshape(window, HD)
    value_part = pieces[1].reshape(window, HD)

    score_scale = 1.0 / math.sqrt(HD)
    allowed = (key_seg[None, :] == query_seg[:, None]) & query_valid[:, None] & (
        key_pos[None, :] <= query_pos[:, None]
    ) | (key_pos[None, :] == query_pos[:, None])
    scores = (
        jnp.einsum("rhd,kd->rhk", queries, key_part, preferred_element_type=jnp.float32)
        * score_scale
    )
    scores = jnp.where(allowed[:, None, :], scores, MASK_FILL)
    new_max = jnp.max(scores, axis=2)
    prob_terms = jnp.where(allowed[:, None, :], jnp.exp(scores - new_max[:, :, None]), 0.0)
    totals = jnp.sum(prob_terms, axis=2)
    accum = jnp.einsum(
        "rhk,kd->rhd",
        prob_terms.astype(jnp.bfloat16),
        value_part,
        preferred_element_type=jnp.float32,
    )
    attended = (
        (accum / totals[:, :, None]).reshape(local_rows, head_count * HD).astype(jnp.bfloat16)
    )
    return jnp.where(query_valid[:, None], attended, jnp.zeros((), jnp.bfloat16))


def solution(mesh):
    heads_per_kv = QH // KVH
    tp_count = mesh.shape["tp"]
    group_size = heads_per_kv * tp_count // QH
    x_count = 4
    z_count = tp_count // x_count
    devices = mesh.devices.reshape(
        mesh.shape["rep"], mesh.shape["seq"], x_count, z_count // group_size, group_size
    )
    grid = jax.sharding.Mesh(devices, ("rep", "seq", "x", "zh", "zl"))
    tp = ("x", "zh", "zl")
    in_specs = (
        P("rep", ("seq",) + tp),
        P(),
        P("seq", tp),
        P(None, tp, None),
        P(),
        P(),
    )
    out_specs = P(("rep", "seq"), tp)
    return jax.shard_map(local, mesh=grid, in_specs=in_specs, out_specs=out_specs, check_vma=False)
```

```python
import math

import jax
import jax.numpy as jnp
from jax import lax
from jax.sharding import PartitionSpec as P

D = 8192
QH = 64
KVH = 8
HD = 128
RESP = 2
LMAX = 192
LMIN = 128
BUFFER = 384


ROPE_BASE = 500000.0
NORM_EPS = 1e-05
MASK_FILL = -1e30


def response_tables(lengths, routes):
    flat_len = lengths.reshape(-1)
    flat_route = routes.reshape(-1)
    response_ids = jnp.arange(flat_len.shape[0], dtype=jnp.int32)
    group_of = response_ids // RESP
    same_route = flat_route[:, None] == flat_route[None, :]
    same_group = group_of[:, None] == group_of[None, :]
    earlier = response_ids[None, :] < response_ids[:, None]
    dest_off = jnp.sum(jnp.where(same_route & earlier, flat_len[None, :], 0), axis=1)
    pair_off = jnp.sum(jnp.where(same_route & same_group & earlier, flat_len[None, :], 0), axis=1)
    src_start = jnp.sum(jnp.where(same_group & earlier, flat_len[None, :], 0), axis=1)
    return (flat_len, flat_route, group_of, dest_off, pair_off, src_start)


def locate(positions, replica, tables):
    flat_len, flat_route, group_of, dest_off, pair_off, src_start = tables
    response_ids = jnp.arange(flat_len.shape[0], dtype=jnp.int32)
    position_col = positions[:, None]
    inside = (
        (flat_route[None, :] == replica)
        & (dest_off[None, :] <= position_col)
        & (position_col < dest_off[None, :] + flat_len[None, :])
    )
    inside_int = inside.astype(jnp.int32)
    segment = jnp.sum(inside_int * (response_ids[None, :] + 1), axis=1) - 1
    seg_start = jnp.sum(inside_int * dest_off[None, :], axis=1)
    source_group = jnp.sum(inside_int * group_of[None, :], axis=1)
    pair_first = jnp.sum(inside_int * (dest_off - pair_off)[None, :], axis=1)
    source = jnp.sum(inside_int * src_start[None, :], axis=1)
    within = jnp.where(segment >= 0, positions - seg_start, 0)
    return (segment, within, source_group, pair_first, source)


def rotary(values_in, within):
    head_dim = values_in.shape[-1]
    half_dim = head_dim // 2
    freq_index = jnp.arange(half_dim, dtype=jnp.float32)
    inverse = jnp.power(ROPE_BASE, -2.0 * freq_index / head_dim)
    angles = within.astype(jnp.float32)[:, None] * inverse[None, :]
    cosine = jnp.cos(angles)[:, None, :]
    sine_part = jnp.sin(angles)[:, None, :]
    lower_half = values_in[..., :half_dim]
    upper_half = values_in[..., half_dim:]
    return jnp.concatenate(
        [
            lower_half * cosine - upper_half * sine_part,
            upper_half * cosine + lower_half * sine_part,
        ],
        axis=-1,
    )


def fill_rows(table, indices, present):
    taken = jnp.take(table, indices.reshape(-1), axis=0)
    return jnp.where(present.reshape(-1)[:, None], taken, jnp.zeros((), table.dtype))


def local(hidden, gain, w_query, w_keyval, lengths, routes):
    rep_count = lax.axis_size("rep")
    seq_count = lax.axis_size("seq")
    x_count = lax.axis_size("x")
    group_size = lax.axis_size("zl")
    z_count = lax.axis_size("zh") * group_size
    tp_count = x_count * z_count
    replica = lax.axis_index("rep")
    seq_index = lax.axis_index("seq")
    sub = lax.axis_index("zl")
    feature_cols = hidden.shape[1]
    local_rows = BUFFER // seq_count
    head_count = w_query.shape[1] // HD
    kv_cols = 2 * HD // group_size
    quarter = HD // 4

    my_lengths = lax.dynamic_index_in_dim(lengths, replica, 0, keepdims=False)
    my_routes = lax.dynamic_index_in_dim(routes, replica, 0, keepdims=False)
    first_block = hidden[:LMAX]
    second_block = lax.dynamic_slice_in_dim(hidden, my_lengths[0], LMAX, 0)
    targets = jnp.arange(rep_count, dtype=jnp.int32)
    outgoing = jnp.where(
        (targets == my_routes[0])[:, None, None], first_block[None], second_block[None]
    ).reshape(rep_count * LMAX, feature_cols)
    w_half = lax.dynamic_index_in_dim(w_keyval, seq_index, 0, keepdims=False)
    w_half = w_half.reshape(feature_cols, KVH, 2, 2, 2, quarter)
    w_half = w_half.transpose(1, 2, 4, 0, 3, 5).reshape(tp_count, feature_cols, kv_cols)
    w_kv = lax.all_to_all(w_half, ("x", "zh", "zl"), split_axis=0, concat_axis=0, tiled=True)
    incoming = lax.all_to_all(outgoing, "rep", split_axis=0, concat_axis=0, tiled=True)
    w_kv = w_kv.reshape(x_count, z_count, feature_cols, kv_cols)
    tables = response_tables(lengths, routes)
    all_pos = jnp.arange(BUFFER, dtype=jnp.int32)
    segment, within, source_group, pair_first, source = locate(all_pos, replica, tables)
    valid = segment >= 0
    gathered_idx = jnp.where(valid, source_group * LMAX + all_pos - pair_first, 0)
    assembled = fill_rows(incoming, gathered_idx, valid)

    spread = jnp.broadcast_to(assembled[None], (x_count,) + assembled.shape)
    gathered = lax.all_to_all(spread, "x", split_axis=0, concat_axis=0, tiled=True)
    gathered = lax.all_gather(gathered, ("zh", "zl"), axis=0, tiled=False)
    gain_half = lax.dynamic_index_in_dim(
        gain.reshape(seq_count, x_count, z_count, feature_cols), seq_index, 0, keepdims=False
    )
    gathered_f = gathered.astype(jnp.float32)
    scaled = (gathered_f * gain_half.transpose(1, 0, 2)[:, :, None, :]).astype(jnp.bfloat16)
    squares = jnp.sum(gathered_f * gathered_f, axis=(0, 1, 3))
    w_q = w_query.reshape(x_count, z_count, feature_cols, w_query.shape[1])
    both = jnp.einsum(
        "zxri,xzic->rc",
        scaled,
        jnp.concatenate([w_q, w_kv], axis=3),
        preferred_element_type=jnp.float32,
    )
    query_part = both[:, : w_q.shape[3]]
    kv_part = both[:, w_q.shape[3] :]

    window = BUFFER - LMIN
    rest = BUFFER - window
    partner = seq_count - 1 - seq_index
    query_cols = query_part.shape[1]
    payload = jnp.concatenate(
        [
            lax.dynamic_slice_in_dim(query_part, partner * local_rows, local_rows, 0).reshape(-1),
            lax.dynamic_slice_in_dim(kv_part, partner * rest, window, 0).reshape(-1),
            lax.dynamic_slice_in_dim(squares, partner * rest, window),
        ]
    )
    got = lax.ppermute(payload, "seq", perm=[(0, 1), (1, 0)])
    q_size = local_rows * query_cols
    kv_size = window * kv_cols
    win_at = seq_index * rest
    query_at = seq_index * local_rows
    query_raw = lax.dynamic_slice_in_dim(query_part, query_at, local_rows, 0) + got[
        :q_size
    ].reshape(local_rows, query_cols)
    kv_raw = lax.dynamic_slice_in_dim(kv_part, win_at, window, 0) + got[
        q_size : q_size + kv_size
    ].reshape(window, kv_cols)
    win_squares = lax.dynamic_slice_in_dim(squares, win_at, window) + got[q_size + kv_size :]
    win_rms = lax.rsqrt(win_squares / D + NORM_EPS)
    query_rms = lax.dynamic_slice_in_dim(win_rms, query_at - win_at, local_rows)

    query_pos = query_at + jnp.arange(local_rows, dtype=jnp.int32)
    query_seg = lax.dynamic_slice_in_dim(segment, query_at, local_rows)
    query_within = lax.dynamic_slice_in_dim(within, query_at, local_rows)
    query_valid = query_seg >= 0
    queries = rotary(
        query_rms[:, None, None] * query_raw.reshape(local_rows, head_count, HD), query_within
    ).astype(jnp.bfloat16)

    key_pos = win_at + jnp.arange(window, dtype=jnp.int32)
    key_seg = lax.dynamic_slice_in_dim(segment, win_at, window)
    key_within = lax.dynamic_slice_in_dim(within, win_at, window)
    kv_scaled = (win_rms[:, None] * kv_raw).reshape(window, 2, quarter)
    freq_index = (sub % 2 * quarter + jnp.arange(quarter, dtype=jnp.int32)).astype(jnp.float32)
    inverse = jnp.power(ROPE_BASE, -2.0 * freq_index / HD)
    angles = key_within.astype(jnp.float32)[:, None] * inverse[None, :]
    cosine = jnp.cos(angles)
    sine_part = jnp.sin(angles)
    lower_half = kv_scaled[:, 0]
    upper_half = kv_scaled[:, 1]
    roped = jnp.stack(
        [lower_half * cosine - upper_half * sine_part, upper_half * cosine + lower_half * sine_part],
        axis=1,
    )
    piece = jnp.where(sub < 2, roped, kv_scaled).astype(jnp.bfloat16)
    spread = jnp.broadcast_to(piece[None], (group_size,) + piece.shape)
    pieces = lax.all_to_all(spread, "zl", split_axis=0, concat_axis=0, tiled=True)
    pieces = pieces.reshape(2, 2, window, 2, quarter).transpose(0, 2, 3, 1, 4)
    key_part = pieces[0].reshape(window, HD)
    value_part = pieces[1].reshape(window, HD)

    score_scale = 1.0 / math.sqrt(HD)
    allowed = (key_seg[None, :] == query_seg[:, None]) & query_valid[:, None] & (
        key_pos[None, :] <= query_pos[:, None]
    ) | (key_pos[None, :] == query_pos[:, None])
    scores = (
        jnp.einsum("rhd,kd->rhk", queries, key_part, preferred_element_type=jnp.float32)
        * score_scale
    )
    scores = jnp.where(allowed[:, None, :], scores, MASK_FILL)
    new_max = jnp.max(scores, axis=2)
    prob_terms = jnp.where(allowed[:, None, :], jnp.exp(scores - new_max[:, :, None]), 0.0)
    totals = jnp.sum(prob_terms, axis=2)
    accum = jnp.einsum(
        "rhk,kd->rhd",
        prob_terms.astype(jnp.bfloat16),
        value_part,
        preferred_element_type=jnp.float32,
    )
    attended = (
        (accum / totals[:, :, None]).reshape(local_rows, head_count * HD).astype(jnp.bfloat16)
    )
    return jnp.where(query_valid[:, None], attended, jnp.zeros((), jnp.bfloat16))


def solution(mesh):
    heads_per_kv = QH // KVH
    tp_count = mesh.shape["tp"]
    group_size = heads_per_kv * tp_count // QH
    x_count = 4
    z_count = tp_count // x_count
    devices = mesh.devices.reshape(
        mesh.shape["rep"], mesh.shape["seq"], x_count, z_count // group_size, group_size
    )
    grid = jax.sharding.Mesh(devices, ("rep", "seq", "x", "zh", "zl"))
    tp = ("x", "zh", "zl")
    in_specs = (
        P("rep", ("seq",) + tp),
        P(),
        P("seq", tp),
        P(None, tp, None),
        P(),
        P(),
    )
    out_specs = P(("rep", "seq"), tp)
    return jax.shard_map(local, mesh=grid, in_specs=in_specs, out_specs=out_specs, check_vma=False)
```

```python
import math

import jax
import jax.numpy as jnp
from jax import lax
from jax.sharding import PartitionSpec as P

D = 8192
QH = 64
KVH = 8
HD = 128
RESP = 2
LMAX = 192
LMIN = 128
BUFFER = 384


ROPE_BASE = 500000.0
NORM_EPS = 1e-05
MASK_FILL = -1e30


def response_tables(lengths, routes):
    flat_len = lengths.reshape(-1)
    flat_route = routes.reshape(-1)
    response_ids = jnp.arange(flat_len.shape[0], dtype=jnp.int32)
    group_of = response_ids // RESP
    same_route = flat_route[:, None] == flat_route[None, :]
    same_group = group_of[:, None] == group_of[None, :]
    earlier = response_ids[None, :] < response_ids[:, None]
    dest_off = jnp.sum(jnp.where(same_route & earlier, flat_len[None, :], 0), axis=1)
    pair_off = jnp.sum(jnp.where(same_route & same_group & earlier, flat_len[None, :], 0), axis=1)
    src_start = jnp.sum(jnp.where(same_group & earlier, flat_len[None, :], 0), axis=1)
    return (flat_len, flat_route, group_of, dest_off, pair_off, src_start)


def locate(positions, replica, tables):
    flat_len, flat_route, group_of, dest_off, pair_off, src_start = tables
    response_ids = jnp.arange(flat_len.shape[0], dtype=jnp.int32)
    position_col = positions[:, None]
    inside = (
        (flat_route[None, :] == replica)
        & (dest_off[None, :] <= position_col)
        & (position_col < dest_off[None, :] + flat_len[None, :])
    )
    inside_int = inside.astype(jnp.int32)
    segment = jnp.sum(inside_int * (response_ids[None, :] + 1), axis=1) - 1
    seg_start = jnp.sum(inside_int * dest_off[None, :], axis=1)
    source_group = jnp.sum(inside_int * group_of[None, :], axis=1)
    pair_first = jnp.sum(inside_int * (dest_off - pair_off)[None, :], axis=1)
    source = jnp.sum(inside_int * src_start[None, :], axis=1)
    within = jnp.where(segment >= 0, positions - seg_start, 0)
    return (segment, within, source_group, pair_first, source)


def rotary(values_in, within):
    head_dim = values_in.shape[-1]
    half_dim = head_dim // 2
    freq_index = jnp.arange(half_dim, dtype=jnp.float32)
    inverse = jnp.power(ROPE_BASE, -2.0 * freq_index / head_dim)
    angles = within.astype(jnp.float32)[:, None] * inverse[None, :]
    cosine = jnp.cos(angles)[:, None, :]
    sine_part = jnp.sin(angles)[:, None, :]
    lower_half = values_in[..., :half_dim]
    upper_half = values_in[..., half_dim:]
    return jnp.concatenate(
        [
            lower_half * cosine - upper_half * sine_part,
            upper_half * cosine + lower_half * sine_part,
        ],
        axis=-1,
    )


def fill_rows(table, indices, present):
    taken = jnp.take(table, indices.reshape(-1), axis=0)
    return jnp.where(present.reshape(-1)[:, None], taken, jnp.zeros((), table.dtype))


def local(hidden, gain, w_query, w_keyval, lengths, routes):
    rep_count = lax.axis_size("rep")
    seq_count = lax.axis_size("seq")
    x_count = lax.axis_size("x")
    group_size = lax.axis_size("zl")
    z_count = lax.axis_size("zh") * group_size
    tp_count = x_count * z_count
    replica = lax.axis_index("rep")
    seq_index = lax.axis_index("seq")
    sub = lax.axis_index("zl")
    feature_cols = hidden.shape[1]
    local_rows = BUFFER // seq_count
    head_count = w_query.shape[1] // HD
    kv_cols = 2 * HD // group_size
    quarter = HD // 4

    my_lengths = lax.dynamic_index_in_dim(lengths, replica, 0, keepdims=False)
    my_routes = lax.dynamic_index_in_dim(routes, replica, 0, keepdims=False)
    first_block = hidden[:LMAX]
    second_block = lax.dynamic_slice_in_dim(hidden, my_lengths[0], LMAX, 0)
    targets = jnp.arange(rep_count, dtype=jnp.int32)
    outgoing = jnp.where(
        (targets == my_routes[0])[:, None, None], first_block[None], second_block[None]
    ).reshape(rep_count * LMAX, feature_cols)
    incoming = lax.all_to_all(outgoing, "rep", split_axis=0, concat_axis=0, tiled=True)
    tables = response_tables(lengths, routes)
    all_pos = jnp.arange(BUFFER, dtype=jnp.int32)
    segment, within, source_group, pair_first, source = locate(all_pos, replica, tables)
    valid = segment >= 0
    gathered_idx = jnp.where(valid, source_group * LMAX + all_pos - pair_first, 0)
    assembled = fill_rows(incoming, gathered_idx, valid)

    spread = jnp.broadcast_to(assembled[None], (x_count,) + assembled.shape)
    gathered = lax.all_to_all(spread, "x", split_axis=0, concat_axis=0, tiled=True)
    gathered = lax.all_gather(gathered, ("zh", "zl"), axis=0, tiled=False)
    gain_half = lax.dynamic_index_in_dim(
        gain.reshape(seq_count, x_count, z_count, feature_cols), seq_index, 0, keepdims=False
    )
    gathered_f = gathered.astype(jnp.float32)
    scaled = (gathered_f * gain_half.transpose(1, 0, 2)[:, :, None, :]).astype(jnp.bfloat16)
    squares = jnp.sum(gathered_f * gathered_f, axis=(0, 1, 3))
    w_q = w_query.reshape(x_count, z_count, feature_cols, w_query.shape[1])
    query_part = jnp.einsum("zxri,xzic->rc", scaled, w_q, preferred_element_type=jnp.float32)

    window = BUFFER - LMIN
    rest = BUFFER - window
    partner = seq_count - 1 - seq_index
    query_cols = query_part.shape[1]
    win_at = seq_index * rest
    query_at = seq_index * local_rows
    payload = jnp.concatenate(
        [
            lax.dynamic_slice_in_dim(query_part, partner * local_rows, local_rows, 0),
            lax.dynamic_slice_in_dim(squares, partner * rest, window).reshape(-1, query_cols),
        ],
        axis=0,
    )
    got = lax.ppermute(payload, "seq", perm=[(0, 1), (1, 0)])

    w_half = lax.dynamic_index_in_dim(w_keyval, seq_index, 0, keepdims=False)
    w_half = w_half.reshape(feature_cols, KVH, 2, 2, 2, quarter)
    w_half = w_half.transpose(1, 2, 4, 0, 3, 5).reshape(tp_count, feature_cols, kv_cols)
    w_half, scaled = lax.optimization_barrier((w_half, scaled))
    w_kv = lax.all_to_all(w_half, ("x", "zh", "zl"), split_axis=0, concat_axis=0, tiled=True)
    w_kv = w_kv.reshape(x_count, z_count, feature_cols, kv_cols)
    kv_part = jnp.einsum("zxri,xzic->rc", scaled, w_kv, preferred_element_type=jnp.float32)
    got_kv = lax.ppermute(
        lax.dynamic_slice_in_dim(kv_part, partner * rest, window, 0), "seq", perm=[(0, 1), (1, 0)]
    )
    query_raw = lax.dynamic_slice_in_dim(query_part, query_at, local_rows, 0) + got[:local_rows]
    kv_raw = lax.dynamic_slice_in_dim(kv_part, win_at, window, 0) + got_kv
    win_squares = lax.dynamic_slice_in_dim(squares, win_at, window) + got[local_rows:].reshape(-1)
    win_rms = lax.rsqrt(win_squares / D + NORM_EPS)
    query_rms = lax.dynamic_slice_in_dim(win_rms, query_at - win_at, local_rows)

    query_pos = query_at + jnp.arange(local_rows, dtype=jnp.int32)
    query_seg = lax.dynamic_slice_in_dim(segment, query_at, local_rows)
    query_within = lax.dynamic_slice_in_dim(within, query_at, local_rows)
    query_valid = query_seg >= 0
    queries = rotary(
        query_rms[:, None, None] * query_raw.reshape(local_rows, head_count, HD), query_within
    ).astype(jnp.bfloat16)

    key_pos = win_at + jnp.arange(window, dtype=jnp.int32)
    key_seg = lax.dynamic_slice_in_dim(segment, win_at, window)
    key_within = lax.dynamic_slice_in_dim(within, win_at, window)
    kv_scaled = (win_rms[:, None] * kv_raw).reshape(window, 2, quarter)
    freq_index = (sub % 2 * quarter + jnp.arange(quarter, dtype=jnp.int32)).astype(jnp.float32)
    inverse = jnp.power(ROPE_BASE, -2.0 * freq_index / HD)
    angles = key_within.astype(jnp.float32)[:, None] * inverse[None, :]
    cosine = jnp.cos(angles)
    sine_part = jnp.sin(angles)
    lower_half = kv_scaled[:, 0]
    upper_half = kv_scaled[:, 1]
    roped = jnp.stack(
        [lower_half * cosine - upper_half * sine_part, upper_half * cosine + lower_half * sine_part],
        axis=1,
    )
    piece = jnp.where(sub < 2, roped, kv_scaled).astype(jnp.bfloat16)
    spread = jnp.broadcast_to(piece[None], (group_size,) + piece.shape)
    pieces = lax.all_to_all(spread, "zl", split_axis=0, concat_axis=0, tiled=True)
    pieces = pieces.reshape(2, 2, window, 2, quarter).transpose(0, 2, 3, 1, 4)
    key_part = pieces[0].reshape(window, HD)
    value_part = pieces[1].reshape(window, HD)

    score_scale = 1.0 / math.sqrt(HD)
    allowed = (key_seg[None, :] == query_seg[:, None]) & query_valid[:, None] & (
        key_pos[None, :] <= query_pos[:, None]
    ) | (key_pos[None, :] == query_pos[:, None])
    scores = (
        jnp.einsum("rhd,kd->rhk", queries, key_part, preferred_element_type=jnp.float32)
        * score_scale
    )
    scores = jnp.where(allowed[:, None, :], scores, MASK_FILL)
    new_max = jnp.max(scores, axis=2)
    prob_terms = jnp.where(allowed[:, None, :], jnp.exp(scores - new_max[:, :, None]), 0.0)
    totals = jnp.sum(prob_terms, axis=2)
    accum = jnp.einsum(
        "rhk,kd->rhd",
        prob_terms.astype(jnp.bfloat16),
        value_part,
        preferred_element_type=jnp.float32,
    )
    attended = (
        (accum / totals[:, :, None]).reshape(local_rows, head_count * HD).astype(jnp.bfloat16)
    )
    return jnp.where(query_valid[:, None], attended, jnp.zeros((), jnp.bfloat16))


def solution(mesh):
    heads_per_kv = QH // KVH
    tp_count = mesh.shape["tp"]
    group_size = heads_per_kv * tp_count // QH
    x_count = 4
    z_count = tp_count // x_count
    devices = mesh.devices.reshape(
        mesh.shape["rep"], mesh.shape["seq"], x_count, z_count // group_size, group_size
    )
    grid = jax.sharding.Mesh(devices, ("rep", "seq", "x", "zh", "zl"))
    tp = ("x", "zh", "zl")
    in_specs = (
        P("rep", ("seq",) + tp),
        P(),
        P("seq", tp),
        P(None, tp, None),
        P(),
        P(),
    )
    out_specs = P(("rep", "seq"), tp)
    return jax.shard_map(local, mesh=grid, in_specs=in_specs, out_specs=out_specs, check_vma=False)
```

```python
import math

import jax
import jax.numpy as jnp
from jax import lax
from jax.sharding import PartitionSpec as P

D = 8192
QH = 64
KVH = 8
HD = 128
RESP = 2
LMAX = 192
LMIN = 128
BUFFER = 384


ROPE_BASE = 500000.0
NORM_EPS = 1e-05
MASK_FILL = -1e30


def response_tables(lengths, routes):
    flat_len = lengths.reshape(-1)
    flat_route = routes.reshape(-1)
    response_ids = jnp.arange(flat_len.shape[0], dtype=jnp.int32)
    group_of = response_ids // RESP
    same_route = flat_route[:, None] == flat_route[None, :]
    same_group = group_of[:, None] == group_of[None, :]
    earlier = response_ids[None, :] < response_ids[:, None]
    dest_off = jnp.sum(jnp.where(same_route & earlier, flat_len[None, :], 0), axis=1)
    pair_off = jnp.sum(jnp.where(same_route & same_group & earlier, flat_len[None, :], 0), axis=1)
    src_start = jnp.sum(jnp.where(same_group & earlier, flat_len[None, :], 0), axis=1)
    return (flat_len, flat_route, group_of, dest_off, pair_off, src_start)


def locate(positions, replica, tables):
    flat_len, flat_route, group_of, dest_off, pair_off, src_start = tables
    response_ids = jnp.arange(flat_len.shape[0], dtype=jnp.int32)
    position_col = positions[:, None]
    inside = (
        (flat_route[None, :] == replica)
        & (dest_off[None, :] <= position_col)
        & (position_col < dest_off[None, :] + flat_len[None, :])
    )
    inside_int = inside.astype(jnp.int32)
    segment = jnp.sum(inside_int * (response_ids[None, :] + 1), axis=1) - 1
    seg_start = jnp.sum(inside_int * dest_off[None, :], axis=1)
    source_group = jnp.sum(inside_int * group_of[None, :], axis=1)
    pair_first = jnp.sum(inside_int * (dest_off - pair_off)[None, :], axis=1)
    source = jnp.sum(inside_int * src_start[None, :], axis=1)
    within = jnp.where(segment >= 0, positions - seg_start, 0)
    return (segment, within, source_group, pair_first, source)


def rotary(values_in, within):
    head_dim = values_in.shape[-1]
    half_dim = head_dim // 2
    freq_index = jnp.arange(half_dim, dtype=jnp.float32)
    inverse = jnp.power(ROPE_BASE, -2.0 * freq_index / head_dim)
    angles = within.astype(jnp.float32)[:, None] * inverse[None, :]
    cosine = jnp.cos(angles)[:, None, :]
    sine_part = jnp.sin(angles)[:, None, :]
    lower_half = values_in[..., :half_dim]
    upper_half = values_in[..., half_dim:]
    return jnp.concatenate(
        [
            lower_half * cosine - upper_half * sine_part,
            upper_half * cosine + lower_half * sine_part,
        ],
        axis=-1,
    )


def fill_rows(table, indices, present):
    taken = jnp.take(table, indices.reshape(-1), axis=0)
    return jnp.where(present.reshape(-1)[:, None], taken, jnp.zeros((), table.dtype))


def local(hidden, gain, w_query, w_keyval, lengths, routes):
    rep_count = lax.axis_size("rep")
    seq_count = lax.axis_size("seq")
    x_count = lax.axis_size("x")
    group_size = lax.axis_size("zl")
    z_count = lax.axis_size("zh") * group_size
    tp_count = x_count * z_count
    replica = lax.axis_index("rep")
    seq_index = lax.axis_index("seq")
    sub = lax.axis_index("zl")
    feature_cols = hidden.shape[1]
    local_rows = BUFFER // seq_count
    head_count = w_query.shape[1] // HD
    kv_cols = 2 * HD // group_size
    quarter = HD // 4

    my_lengths = lax.dynamic_index_in_dim(lengths, replica, 0, keepdims=False)
    my_routes = lax.dynamic_index_in_dim(routes, replica, 0, keepdims=False)
    first_block = hidden[:LMAX]
    second_block = lax.dynamic_slice_in_dim(hidden, my_lengths[0], LMAX, 0)
    targets = jnp.arange(rep_count, dtype=jnp.int32)
    outgoing = jnp.where(
        (targets == my_routes[0])[:, None, None], first_block[None], second_block[None]
    ).reshape(rep_count * LMAX, feature_cols)
    core = replica % 2
    eighth = quarter // 2
    w_half = lax.dynamic_index_in_dim(w_keyval, seq_index, 0, keepdims=False)
    w_half = w_half.reshape(feature_cols, KVH, 2, 2, 2, 2, eighth)
    w_half = lax.dynamic_index_in_dim(w_half, core, 5, keepdims=False)
    w_half = w_half.transpose(1, 2, 4, 0, 3, 5).reshape(tp_count, feature_cols, kv_cols // 2)
    w_mine = lax.all_to_all(w_half, ("x", "zh", "zl"), split_axis=0, concat_axis=0, tiled=True)
    w_other = lax.ppermute(
        w_mine, "rep", perm=[(i, i + 1 - 2 * (i % 2)) for i in range(rep_count)]
    )
    w_kv = jnp.where(core == 0, jnp.stack([w_mine, w_other]), jnp.stack([w_other, w_mine]))
    w_kv = w_kv.reshape(2, tp_count, feature_cols, 2, eighth).transpose(1, 2, 3, 0, 4)
    incoming = lax.all_to_all(outgoing, "rep", split_axis=0, concat_axis=0, tiled=True)
    w_kv = w_kv.reshape(x_count, z_count, feature_cols, kv_cols)
    tables = response_tables(lengths, routes)
    all_pos = jnp.arange(BUFFER, dtype=jnp.int32)
    segment, within, source_group, pair_first, source = locate(all_pos, replica, tables)
    valid = segment >= 0
    gathered_idx = jnp.where(valid, source_group * LMAX + all_pos - pair_first, 0)
    assembled = fill_rows(incoming, gathered_idx, valid)

    spread = jnp.broadcast_to(assembled[None], (x_count,) + assembled.shape)
    gathered = lax.all_to_all(spread, "x", split_axis=0, concat_axis=0, tiled=True)
    gathered = lax.all_gather(gathered, ("zh", "zl"), axis=0, tiled=False)
    gain_half = lax.dynamic_index_in_dim(
        gain.reshape(seq_count, x_count, z_count, feature_cols), seq_index, 0, keepdims=False
    )
    gathered_f = gathered.astype(jnp.float32)
    scaled = (gathered_f * gain_half.transpose(1, 0, 2)[:, :, None, :]).astype(jnp.bfloat16)
    squares = jnp.sum(gathered_f * gathered_f, axis=(0, 1, 3))
    w_q = w_query.reshape(x_count, z_count, feature_cols, w_query.shape[1])
    query_part = jnp.einsum("zxri,xzic->rc", scaled, w_q, preferred_element_type=jnp.float32)
    kv_part = jnp.einsum("zxri,xzic->rc", scaled, w_kv, preferred_element_type=jnp.float32)

    window = BUFFER - LMIN
    rest = BUFFER - window
    partner = seq_count - 1 - seq_index
    query_cols = query_part.shape[1]
    payload = jnp.concatenate(
        [
            lax.dynamic_slice_in_dim(query_part, partner * local_rows, local_rows, 0).reshape(-1),
            lax.dynamic_slice_in_dim(kv_part, partner * rest, window, 0).reshape(-1),
            lax.dynamic_slice_in_dim(squares, partner * rest, window),
        ]
    )
    got = lax.ppermute(payload, "seq", perm=[(0, 1), (1, 0)])
    q_size = local_rows * query_cols
    kv_size = window * kv_cols
    win_at = seq_index * rest
    query_at = seq_index * local_rows
    query_raw = lax.dynamic_slice_in_dim(query_part, query_at, local_rows, 0) + got[
        :q_size
    ].reshape(local_rows, query_cols)
    kv_raw = lax.dynamic_slice_in_dim(kv_part, win_at, window, 0) + got[
        q_size : q_size + kv_size
    ].reshape(window, kv_cols)
    win_squares = lax.dynamic_slice_in_dim(squares, win_at, window) + got[q_size + kv_size :]
    win_rms = lax.rsqrt(win_squares / D + NORM_EPS)
    query_rms = lax.dynamic_slice_in_dim(win_rms, query_at - win_at, local_rows)

    query_pos = query_at + jnp.arange(local_rows, dtype=jnp.int32)
    query_seg = lax.dynamic_slice_in_dim(segment, query_at, local_rows)
    query_within = lax.dynamic_slice_in_dim(within, query_at, local_rows)
    query_valid = query_seg >= 0
    queries = rotary(
        query_rms[:, None, None] * query_raw.reshape(local_rows, head_count, HD), query_within
    ).astype(jnp.bfloat16)

    key_pos = win_at + jnp.arange(window, dtype=jnp.int32)
    key_seg = lax.dynamic_slice_in_dim(segment, win_at, window)
    key_within = lax.dynamic_slice_in_dim(within, win_at, window)
    kv_scaled = (win_rms[:, None] * kv_raw).reshape(window, 2, quarter)
    freq_index = (sub % 2 * quarter + jnp.arange(quarter, dtype=jnp.int32)).astype(jnp.float32)
    inverse = jnp.power(ROPE_BASE, -2.0 * freq_index / HD)
    angles = key_within.astype(jnp.float32)[:, None] * inverse[None, :]
    cosine = jnp.cos(angles)
    sine_part = jnp.sin(angles)
    lower_half = kv_scaled[:, 0]
    upper_half = kv_scaled[:, 1]
    roped = jnp.stack(
        [lower_half * cosine - upper_half * sine_part, upper_half * cosine + lower_half * sine_part],
        axis=1,
    )
    piece = jnp.where(sub < 2, roped, kv_scaled).astype(jnp.bfloat16)
    spread = jnp.broadcast_to(piece[None], (group_size,) + piece.shape)
    pieces = lax.all_to_all(spread, "zl", split_axis=0, concat_axis=0, tiled=True)
    pieces = pieces.reshape(2, 2, window, 2, quarter).transpose(0, 2, 3, 1, 4)
    key_part = pieces[0].reshape(window, HD)
    value_part = pieces[1].reshape(window, HD)

    score_scale = 1.0 / math.sqrt(HD)
    allowed = (key_seg[None, :] == query_seg[:, None]) & query_valid[:, None] & (
        key_pos[None, :] <= query_pos[:, None]
    ) | (key_pos[None, :] == query_pos[:, None])
    scores = (
        jnp.einsum("rhd,kd->rhk", queries, key_part, preferred_element_type=jnp.float32)
        * score_scale
    )
    scores = jnp.where(allowed[:, None, :], scores, MASK_FILL)
    new_max = jnp.max(scores, axis=2)
    prob_terms = jnp.where(allowed[:, None, :], jnp.exp(scores - new_max[:, :, None]), 0.0)
    totals = jnp.sum(prob_terms, axis=2)
    accum = jnp.einsum(
        "rhk,kd->rhd",
        prob_terms.astype(jnp.bfloat16),
        value_part,
        preferred_element_type=jnp.float32,
    )
    attended = (
        (accum / totals[:, :, None]).reshape(local_rows, head_count * HD).astype(jnp.bfloat16)
    )
    return jnp.where(query_valid[:, None], attended, jnp.zeros((), jnp.bfloat16))


def solution(mesh):
    heads_per_kv = QH // KVH
    tp_count = mesh.shape["tp"]
    group_size = heads_per_kv * tp_count // QH
    x_count = 4
    z_count = tp_count // x_count
    devices = mesh.devices.reshape(
        mesh.shape["rep"], mesh.shape["seq"], x_count, z_count // group_size, group_size
    )
    grid = jax.sharding.Mesh(devices, ("rep", "seq", "x", "zh", "zl"))
    tp = ("x", "zh", "zl")
    in_specs = (
        P("rep", ("seq",) + tp),
        P(),
        P("seq", tp),
        P(None, tp, None),
        P(),
        P(),
    )
    out_specs = P(("rep", "seq"), tp)
    return jax.shard_map(local, mesh=grid, in_specs=in_specs, out_specs=out_specs, check_vma=False)
```

```python
import math

import jax
import jax.numpy as jnp
from jax import lax
from jax.sharding import PartitionSpec as P

D = 8192
QH = 64
KVH = 8
HD = 128
RESP = 2
LMAX = 192
LMIN = 128
BUFFER = 384


ROPE_BASE = 500000.0
NORM_EPS = 1e-05
MASK_FILL = -1e30


def response_tables(lengths, routes):
    flat_len = lengths.reshape(-1)
    flat_route = routes.reshape(-1)
    response_ids = jnp.arange(flat_len.shape[0], dtype=jnp.int32)
    group_of = response_ids // RESP
    same_route = flat_route[:, None] == flat_route[None, :]
    same_group = group_of[:, None] == group_of[None, :]
    earlier = response_ids[None, :] < response_ids[:, None]
    dest_off = jnp.sum(jnp.where(same_route & earlier, flat_len[None, :], 0), axis=1)
    pair_off = jnp.sum(jnp.where(same_route & same_group & earlier, flat_len[None, :], 0), axis=1)
    src_start = jnp.sum(jnp.where(same_group & earlier, flat_len[None, :], 0), axis=1)
    return (flat_len, flat_route, group_of, dest_off, pair_off, src_start)


def locate(positions, replica, tables):
    flat_len, flat_route, group_of, dest_off, pair_off, src_start = tables
    response_ids = jnp.arange(flat_len.shape[0], dtype=jnp.int32)
    position_col = positions[:, None]
    inside = (
        (flat_route[None, :] == replica)
        & (dest_off[None, :] <= position_col)
        & (position_col < dest_off[None, :] + flat_len[None, :])
    )
    inside_int = inside.astype(jnp.int32)
    segment = jnp.sum(inside_int * (response_ids[None, :] + 1), axis=1) - 1
    seg_start = jnp.sum(inside_int * dest_off[None, :], axis=1)
    source_group = jnp.sum(inside_int * group_of[None, :], axis=1)
    pair_first = jnp.sum(inside_int * (dest_off - pair_off)[None, :], axis=1)
    source = jnp.sum(inside_int * src_start[None, :], axis=1)
    within = jnp.where(segment >= 0, positions - seg_start, 0)
    return (segment, within, source_group, pair_first, source)


def rotary(values_in, within):
    head_dim = values_in.shape[-1]
    half_dim = head_dim // 2
    freq_index = jnp.arange(half_dim, dtype=jnp.float32)
    inverse = jnp.power(ROPE_BASE, -2.0 * freq_index / head_dim)
    angles = within.astype(jnp.float32)[:, None] * inverse[None, :]
    cosine = jnp.cos(angles)[:, None, :]
    sine_part = jnp.sin(angles)[:, None, :]
    lower_half = values_in[..., :half_dim]
    upper_half = values_in[..., half_dim:]
    return jnp.concatenate(
        [
            lower_half * cosine - upper_half * sine_part,
            upper_half * cosine + lower_half * sine_part,
        ],
        axis=-1,
    )


def fill_rows(table, indices, present):
    taken = jnp.take(table, indices.reshape(-1), axis=0)
    return jnp.where(present.reshape(-1)[:, None], taken, jnp.zeros((), table.dtype))


def local(hidden, gain, w_query, w_keyval, lengths, routes):
    rep_count = lax.axis_size("rep")
    seq_count = lax.axis_size("seq")
    x_count = lax.axis_size("x")
    group_size = lax.axis_size("zl")
    z_count = lax.axis_size("zh") * group_size
    tp_count = x_count * z_count
    replica = lax.axis_index("rep")
    seq_index = lax.axis_index("seq")
    sub = lax.axis_index("zl")
    feature_cols = hidden.shape[1]
    local_rows = BUFFER // seq_count
    head_count = w_query.shape[1] // HD
    kv_cols = 2 * HD // group_size
    quarter = HD // 4

    my_lengths = lax.dynamic_index_in_dim(lengths, replica, 0, keepdims=False)
    my_routes = lax.dynamic_index_in_dim(routes, replica, 0, keepdims=False)
    first_block = hidden[:LMAX]
    second_block = lax.dynamic_slice_in_dim(hidden, my_lengths[0], LMAX, 0)
    targets = jnp.arange(rep_count, dtype=jnp.int32)
    outgoing = jnp.where(
        (targets == my_routes[0])[:, None, None], first_block[None], second_block[None]
    ).reshape(rep_count * LMAX, feature_cols)
    slice_cols = quarter // rep_count
    w_half = lax.dynamic_index_in_dim(w_keyval, seq_index, 0, keepdims=False)
    w_half = w_half.reshape(feature_cols, KVH, 2, 2, 2, rep_count, slice_cols)
    w_half = lax.dynamic_index_in_dim(w_half, replica, 5, keepdims=False)
    w_half = w_half.transpose(1, 2, 4, 0, 3, 5).reshape(tp_count, feature_cols, 2 * slice_cols)
    w_mine = lax.all_to_all(w_half, ("x", "zh", "zl"), split_axis=0, concat_axis=0, tiled=True)
    w_spread = jnp.broadcast_to(w_mine[None], (rep_count,) + w_mine.shape)
    w_kv = lax.all_to_all(w_spread, "rep", split_axis=0, concat_axis=0, tiled=True)
    w_kv = w_kv.reshape(rep_count, tp_count, feature_cols, 2, slice_cols).transpose(1, 2, 3, 0, 4)
    incoming = lax.all_to_all(outgoing, "rep", split_axis=0, concat_axis=0, tiled=True)
    w_kv = w_kv.reshape(x_count, z_count, feature_cols, kv_cols)
    tables = response_tables(lengths, routes)
    all_pos = jnp.arange(BUFFER, dtype=jnp.int32)
    segment, within, source_group, pair_first, source = locate(all_pos, replica, tables)
    valid = segment >= 0
    gathered_idx = jnp.where(valid, source_group * LMAX + all_pos - pair_first, 0)
    assembled = fill_rows(incoming, gathered_idx, valid)

    spread = jnp.broadcast_to(assembled[None], (x_count,) + assembled.shape)
    gathered = lax.all_to_all(spread, "x", split_axis=0, concat_axis=0, tiled=True)
    gathered = lax.all_gather(gathered, ("zh", "zl"), axis=0, tiled=False)
    gain_half = lax.dynamic_index_in_dim(
        gain.reshape(seq_count, x_count, z_count, feature_cols), seq_index, 0, keepdims=False
    )
    gathered_f = gathered.astype(jnp.float32)
    scaled = (gathered_f * gain_half.transpose(1, 0, 2)[:, :, None, :]).astype(jnp.bfloat16)
    squares = jnp.sum(gathered_f * gathered_f, axis=(0, 1, 3))
    w_q = w_query.reshape(x_count, z_count, feature_cols, w_query.shape[1])
    query_part = jnp.einsum("zxri,xzic->rc", scaled, w_q, preferred_element_type=jnp.float32)
    kv_part = jnp.einsum("zxri,xzic->rc", scaled, w_kv, preferred_element_type=jnp.float32)

    window = BUFFER - LMIN
    rest = BUFFER - window
    partner = seq_count - 1 - seq_index
    query_cols = query_part.shape[1]
    payload = jnp.concatenate(
        [
            lax.dynamic_slice_in_dim(query_part, partner * local_rows, local_rows, 0).reshape(-1),
            lax.dynamic_slice_in_dim(kv_part, partner * rest, window, 0).reshape(-1),
            lax.dynamic_slice_in_dim(squares, partner * rest, window),
        ]
    )
    got = lax.ppermute(payload, "seq", perm=[(0, 1), (1, 0)])
    q_size = local_rows * query_cols
    kv_size = window * kv_cols
    win_at = seq_index * rest
    query_at = seq_index * local_rows
    query_raw = lax.dynamic_slice_in_dim(query_part, query_at, local_rows, 0) + got[
        :q_size
    ].reshape(local_rows, query_cols)
    kv_raw = lax.dynamic_slice_in_dim(kv_part, win_at, window, 0) + got[
        q_size : q_size + kv_size
    ].reshape(window, kv_cols)
    win_squares = lax.dynamic_slice_in_dim(squares, win_at, window) + got[q_size + kv_size :]
    win_rms = lax.rsqrt(win_squares / D + NORM_EPS)
    query_rms = lax.dynamic_slice_in_dim(win_rms, query_at - win_at, local_rows)

    query_pos = query_at + jnp.arange(local_rows, dtype=jnp.int32)
    query_seg = lax.dynamic_slice_in_dim(segment, query_at, local_rows)
    query_within = lax.dynamic_slice_in_dim(within, query_at, local_rows)
    query_valid = query_seg >= 0
    queries = rotary(
        query_rms[:, None, None] * query_raw.reshape(local_rows, head_count, HD), query_within
    ).astype(jnp.bfloat16)

    key_pos = win_at + jnp.arange(window, dtype=jnp.int32)
    key_seg = lax.dynamic_slice_in_dim(segment, win_at, window)
    key_within = lax.dynamic_slice_in_dim(within, win_at, window)
    kv_scaled = (win_rms[:, None] * kv_raw).reshape(window, 2, quarter)
    freq_index = (sub % 2 * quarter + jnp.arange(quarter, dtype=jnp.int32)).astype(jnp.float32)
    inverse = jnp.power(ROPE_BASE, -2.0 * freq_index / HD)
    angles = key_within.astype(jnp.float32)[:, None] * inverse[None, :]
    cosine = jnp.cos(angles)
    sine_part = jnp.sin(angles)
    lower_half = kv_scaled[:, 0]
    upper_half = kv_scaled[:, 1]
    roped = jnp.stack(
        [lower_half * cosine - upper_half * sine_part, upper_half * cosine + lower_half * sine_part],
        axis=1,
    )
    piece = jnp.where(sub < 2, roped, kv_scaled).astype(jnp.bfloat16)
    spread = jnp.broadcast_to(piece[None], (group_size,) + piece.shape)
    pieces = lax.all_to_all(spread, "zl", split_axis=0, concat_axis=0, tiled=True)
    pieces = pieces.reshape(2, 2, window, 2, quarter).transpose(0, 2, 3, 1, 4)
    key_part = pieces[0].reshape(window, HD)
    value_part = pieces[1].reshape(window, HD)

    score_scale = 1.0 / math.sqrt(HD)
    allowed = (key_seg[None, :] == query_seg[:, None]) & query_valid[:, None] & (
        key_pos[None, :] <= query_pos[:, None]
    ) | (key_pos[None, :] == query_pos[:, None])
    scores = (
        jnp.einsum("rhd,kd->rhk", queries, key_part, preferred_element_type=jnp.float32)
        * score_scale
    )
    scores = jnp.where(allowed[:, None, :], scores, MASK_FILL)
    new_max = jnp.max(scores, axis=2)
    prob_terms = jnp.where(allowed[:, None, :], jnp.exp(scores - new_max[:, :, None]), 0.0)
    totals = jnp.sum(prob_terms, axis=2)
    accum = jnp.einsum(
        "rhk,kd->rhd",
        prob_terms.astype(jnp.bfloat16),
        value_part,
        preferred_element_type=jnp.float32,
    )
    attended = (
        (accum / totals[:, :, None]).reshape(local_rows, head_count * HD).astype(jnp.bfloat16)
    )
    return jnp.where(query_valid[:, None], attended, jnp.zeros((), jnp.bfloat16))


def solution(mesh):
    heads_per_kv = QH // KVH
    tp_count = mesh.shape["tp"]
    group_size = heads_per_kv * tp_count // QH
    x_count = 4
    z_count = tp_count // x_count
    devices = mesh.devices.reshape(
        mesh.shape["rep"], mesh.shape["seq"], x_count, z_count // group_size, group_size
    )
    grid = jax.sharding.Mesh(devices, ("rep", "seq", "x", "zh", "zl"))
    tp = ("x", "zh", "zl")
    in_specs = (
        P("rep", ("seq",) + tp),
        P(),
        P("seq", tp),
        P(None, tp, None),
        P(),
        P(),
    )
    out_specs = P(("rep", "seq"), tp)
    return jax.shard_map(local, mesh=grid, in_specs=in_specs, out_specs=out_specs, check_vma=False)
```

```python
import math

import jax
import jax.numpy as jnp
from jax import lax
from jax.sharding import PartitionSpec as P

D = 8192
QH = 64
KVH = 8
HD = 128
RESP = 2
LMAX = 192
LMIN = 128
BUFFER = 384


ROPE_BASE = 500000.0
NORM_EPS = 1e-05
MASK_FILL = -1e30


def response_tables(lengths, routes):
    flat_len = lengths.reshape(-1)
    flat_route = routes.reshape(-1)
    response_ids = jnp.arange(flat_len.shape[0], dtype=jnp.int32)
    group_of = response_ids // RESP
    same_route = flat_route[:, None] == flat_route[None, :]
    same_group = group_of[:, None] == group_of[None, :]
    earlier = response_ids[None, :] < response_ids[:, None]
    dest_off = jnp.sum(jnp.where(same_route & earlier, flat_len[None, :], 0), axis=1)
    pair_off = jnp.sum(jnp.where(same_route & same_group & earlier, flat_len[None, :], 0), axis=1)
    src_start = jnp.sum(jnp.where(same_group & earlier, flat_len[None, :], 0), axis=1)
    return (flat_len, flat_route, group_of, dest_off, pair_off, src_start)


def locate(positions, replica, tables):
    flat_len, flat_route, group_of, dest_off, pair_off, src_start = tables
    response_ids = jnp.arange(flat_len.shape[0], dtype=jnp.int32)
    position_col = positions[:, None]
    inside = (
        (flat_route[None, :] == replica)
        & (dest_off[None, :] <= position_col)
        & (position_col < dest_off[None, :] + flat_len[None, :])
    )
    inside_int = inside.astype(jnp.int32)
    segment = jnp.sum(inside_int * (response_ids[None, :] + 1), axis=1) - 1
    seg_start = jnp.sum(inside_int * dest_off[None, :], axis=1)
    source_group = jnp.sum(inside_int * group_of[None, :], axis=1)
    pair_first = jnp.sum(inside_int * (dest_off - pair_off)[None, :], axis=1)
    source = jnp.sum(inside_int * src_start[None, :], axis=1)
    within = jnp.where(segment >= 0, positions - seg_start, 0)
    return (segment, within, source_group, pair_first, source)


def rotary(values_in, within):
    head_dim = values_in.shape[-1]
    half_dim = head_dim // 2
    freq_index = jnp.arange(half_dim, dtype=jnp.float32)
    inverse = jnp.power(ROPE_BASE, -2.0 * freq_index / head_dim)
    angles = within.astype(jnp.float32)[:, None] * inverse[None, :]
    cosine = jnp.cos(angles)[:, None, :]
    sine_part = jnp.sin(angles)[:, None, :]
    lower_half = values_in[..., :half_dim]
    upper_half = values_in[..., half_dim:]
    return jnp.concatenate(
        [
            lower_half * cosine - upper_half * sine_part,
            upper_half * cosine + lower_half * sine_part,
        ],
        axis=-1,
    )


def fill_rows(table, indices, present):
    taken = jnp.take(table, indices.reshape(-1), axis=0)
    return jnp.where(present.reshape(-1)[:, None], taken, jnp.zeros((), table.dtype))


def local(hidden, gain, w_query, w_keyval, lengths, routes):
    rep_count = lax.axis_size("rep")
    seq_count = lax.axis_size("seq")
    x_count = lax.axis_size("x")
    group_size = lax.axis_size("zl")
    z_count = lax.axis_size("zh") * group_size
    tp_count = x_count * z_count
    replica = lax.axis_index("rep")
    seq_index = lax.axis_index("seq")
    sub = lax.axis_index("zl")
    feature_cols = hidden.shape[1]
    local_rows = BUFFER // seq_count
    head_count = w_query.shape[1] // HD
    kv_cols = 2 * HD // group_size
    quarter = HD // 4

    my_lengths = lax.dynamic_index_in_dim(lengths, replica, 0, keepdims=False)
    my_routes = lax.dynamic_index_in_dim(routes, replica, 0, keepdims=False)
    first_block = hidden[:LMAX]
    second_block = lax.dynamic_slice_in_dim(hidden, my_lengths[0], LMAX, 0)
    targets = jnp.arange(rep_count, dtype=jnp.int32)
    outgoing = jnp.where(
        (targets == my_routes[0])[:, None, None], first_block[None], second_block[None]
    ).reshape(rep_count * LMAX, feature_cols)
    slice_cols = quarter // rep_count
    w_half = lax.dynamic_index_in_dim(w_keyval, seq_index, 0, keepdims=False)
    w_half = w_half.reshape(feature_cols, KVH, 2, 2, 2, rep_count, slice_cols)
    w_half = lax.dynamic_index_in_dim(w_half, replica, 5, keepdims=False)
    w_half = w_half.transpose(1, 2, 4, 0, 3, 5).reshape(tp_count, feature_cols, 2 * slice_cols)
    w_mine = lax.all_to_all(w_half, ("x", "zh", "zl"), split_axis=0, concat_axis=0, tiled=True)
    w_spread = jnp.broadcast_to(w_mine[None], (rep_count,) + w_mine.shape)
    w_kv = lax.all_to_all(w_spread, "rep", split_axis=0, concat_axis=0, tiled=True)
    w_kv = w_kv.reshape(rep_count, tp_count, feature_cols, 2, slice_cols).transpose(1, 2, 3, 0, 4)
    incoming = lax.all_to_all(outgoing, "rep", split_axis=0, concat_axis=0, tiled=True)
    w_kv = w_kv.reshape(x_count, z_count, feature_cols, kv_cols)
    tables = response_tables(lengths, routes)
    all_pos = jnp.arange(BUFFER, dtype=jnp.int32)
    segment, within, source_group, pair_first, source = locate(all_pos, replica, tables)
    valid = segment >= 0
    gathered_idx = jnp.where(valid, source_group * LMAX + all_pos - pair_first, 0)
    assembled = fill_rows(incoming, gathered_idx, valid)

    spread = jnp.broadcast_to(assembled[None], (x_count,) + assembled.shape)
    gathered = lax.all_to_all(spread, "x", split_axis=0, concat_axis=0, tiled=True)
    gathered = lax.all_gather(gathered, ("zh", "zl"), axis=0, tiled=False)
    gain_half = lax.dynamic_index_in_dim(
        gain.reshape(seq_count, x_count, z_count, feature_cols), seq_index, 0, keepdims=False
    )
    gathered_f = gathered.astype(jnp.float32)
    scaled = (gathered_f * gain_half.transpose(1, 0, 2)[:, :, None, :]).astype(jnp.bfloat16)
    squares = jnp.sum(gathered_f * gathered_f, axis=(0, 1, 3))
    w_q = w_query.reshape(x_count, z_count, feature_cols, w_query.shape[1])
    both = jnp.einsum(
        "zxri,xzic->rc",
        scaled,
        jnp.concatenate([w_q, w_kv], axis=3),
        preferred_element_type=jnp.float32,
    )
    query_part = both[:, : w_q.shape[3]]
    kv_part = both[:, w_q.shape[3] :]

    window = BUFFER - LMIN
    rest = BUFFER - window
    partner = seq_count - 1 - seq_index
    query_cols = query_part.shape[1]
    payload = jnp.concatenate(
        [
            lax.dynamic_slice_in_dim(query_part, partner * local_rows, local_rows, 0).reshape(-1),
            lax.dynamic_slice_in_dim(kv_part, partner * rest, window, 0).reshape(-1),
            lax.dynamic_slice_in_dim(squares, partner * rest, window),
        ]
    )
    got = lax.ppermute(payload, "seq", perm=[(0, 1), (1, 0)])
    q_size = local_rows * query_cols
    kv_size = window * kv_cols
    win_at = seq_index * rest
    query_at = seq_index * local_rows
    query_raw = lax.dynamic_slice_in_dim(query_part, query_at, local_rows, 0) + got[
        :q_size
    ].reshape(local_rows, query_cols)
    kv_raw = lax.dynamic_slice_in_dim(kv_part, win_at, window, 0) + got[
        q_size : q_size + kv_size
    ].reshape(window, kv_cols)
    win_squares = lax.dynamic_slice_in_dim(squares, win_at, window) + got[q_size + kv_size :]
    win_rms = lax.rsqrt(win_squares / D + NORM_EPS)
    query_rms = lax.dynamic_slice_in_dim(win_rms, query_at - win_at, local_rows)

    query_pos = query_at + jnp.arange(local_rows, dtype=jnp.int32)
    query_seg = lax.dynamic_slice_in_dim(segment, query_at, local_rows)
    query_within = lax.dynamic_slice_in_dim(within, query_at, local_rows)
    query_valid = query_seg >= 0
    queries = rotary(
        query_rms[:, None, None] * query_raw.reshape(local_rows, head_count, HD), query_within
    ).astype(jnp.bfloat16)

    key_pos = win_at + jnp.arange(window, dtype=jnp.int32)
    key_seg = lax.dynamic_slice_in_dim(segment, win_at, window)
    key_within = lax.dynamic_slice_in_dim(within, win_at, window)
    kv_scaled = (win_rms[:, None] * kv_raw).reshape(window, 2, quarter)
    freq_index = (sub % 2 * quarter + jnp.arange(quarter, dtype=jnp.int32)).astype(jnp.float32)
    inverse = jnp.power(ROPE_BASE, -2.0 * freq_index / HD)
    angles = key_within.astype(jnp.float32)[:, None] * inverse[None, :]
    cosine = jnp.cos(angles)
    sine_part = jnp.sin(angles)
    lower_half = kv_scaled[:, 0]
    upper_half = kv_scaled[:, 1]
    roped = jnp.stack(
        [lower_half * cosine - upper_half * sine_part, upper_half * cosine + lower_half * sine_part],
        axis=1,
    )
    piece = jnp.where(sub < 2, roped, kv_scaled).astype(jnp.bfloat16)
    spread = jnp.broadcast_to(piece[None], (group_size,) + piece.shape)
    pieces = lax.all_to_all(spread, "zl", split_axis=0, concat_axis=0, tiled=True)
    pieces = pieces.reshape(2, 2, window, 2, quarter).transpose(0, 2, 3, 1, 4)
    key_part = pieces[0].reshape(window, HD)
    value_part = pieces[1].reshape(window, HD)

    score_scale = 1.0 / math.sqrt(HD)
    allowed = (key_seg[None, :] == query_seg[:, None]) & query_valid[:, None] & (
        key_pos[None, :] <= query_pos[:, None]
    ) | (key_pos[None, :] == query_pos[:, None])
    scores = (
        jnp.einsum("rhd,kd->rhk", queries, key_part, preferred_element_type=jnp.float32)
        * score_scale
    )
    scores = jnp.where(allowed[:, None, :], scores, MASK_FILL)
    new_max = jnp.max(scores, axis=2)
    prob_terms = jnp.where(allowed[:, None, :], jnp.exp(scores - new_max[:, :, None]), 0.0)
    totals = jnp.sum(prob_terms, axis=2)
    accum = jnp.einsum(
        "rhk,kd->rhd",
        prob_terms.astype(jnp.bfloat16),
        value_part,
        preferred_element_type=jnp.float32,
    )
    attended = (
        (accum / totals[:, :, None]).reshape(local_rows, head_count * HD).astype(jnp.bfloat16)
    )
    return jnp.where(query_valid[:, None], attended, jnp.zeros((), jnp.bfloat16))


def solution(mesh):
    heads_per_kv = QH // KVH
    tp_count = mesh.shape["tp"]
    group_size = heads_per_kv * tp_count // QH
    x_count = 4
    z_count = tp_count // x_count
    devices = mesh.devices.reshape(
        mesh.shape["rep"], mesh.shape["seq"], x_count, z_count // group_size, group_size
    )
    grid = jax.sharding.Mesh(devices, ("rep", "seq", "x", "zh", "zl"))
    tp = ("x", "zh", "zl")
    in_specs = (
        P("rep", ("seq",) + tp),
        P(),
        P("seq", tp),
        P(None, tp, None),
        P(),
        P(),
    )
    out_specs = P(("rep", "seq"), tp)
    return jax.shard_map(local, mesh=grid, in_specs=in_specs, out_specs=out_specs, check_vma=False)
```

```python
import math

import jax
import jax.numpy as jnp
from jax import lax
from jax.sharding import PartitionSpec as P

D = 8192
QH = 64
KVH = 8
HD = 128
RESP = 2
LMAX = 192
LMIN = 128
BUFFER = 384


ROPE_BASE = 500000.0
NORM_EPS = 1e-05
MASK_FILL = -1e30


def response_tables(lengths, routes):
    flat_len = lengths.reshape(-1)
    flat_route = routes.reshape(-1)
    response_ids = jnp.arange(flat_len.shape[0], dtype=jnp.int32)
    group_of = response_ids // RESP
    same_route = flat_route[:, None] == flat_route[None, :]
    same_group = group_of[:, None] == group_of[None, :]
    earlier = response_ids[None, :] < response_ids[:, None]
    dest_off = jnp.sum(jnp.where(same_route & earlier, flat_len[None, :], 0), axis=1)
    pair_off = jnp.sum(jnp.where(same_route & same_group & earlier, flat_len[None, :], 0), axis=1)
    src_start = jnp.sum(jnp.where(same_group & earlier, flat_len[None, :], 0), axis=1)
    return (flat_len, flat_route, group_of, dest_off, pair_off, src_start)


def locate(positions, replica, tables):
    flat_len, flat_route, group_of, dest_off, pair_off, src_start = tables
    response_ids = jnp.arange(flat_len.shape[0], dtype=jnp.int32)
    position_col = positions[:, None]
    inside = (
        (flat_route[None, :] == replica)
        & (dest_off[None, :] <= position_col)
        & (position_col < dest_off[None, :] + flat_len[None, :])
    )
    inside_int = inside.astype(jnp.int32)
    segment = jnp.sum(inside_int * (response_ids[None, :] + 1), axis=1) - 1
    seg_start = jnp.sum(inside_int * dest_off[None, :], axis=1)
    source_group = jnp.sum(inside_int * group_of[None, :], axis=1)
    pair_first = jnp.sum(inside_int * (dest_off - pair_off)[None, :], axis=1)
    source = jnp.sum(inside_int * src_start[None, :], axis=1)
    within = jnp.where(segment >= 0, positions - seg_start, 0)
    return (segment, within, source_group, pair_first, source)


def rotary(values_in, within):
    head_dim = values_in.shape[-1]
    half_dim = head_dim // 2
    freq_index = jnp.arange(half_dim, dtype=jnp.float32)
    inverse = jnp.power(ROPE_BASE, -2.0 * freq_index / head_dim)
    angles = within.astype(jnp.float32)[:, None] * inverse[None, :]
    cosine = jnp.cos(angles)[:, None, :]
    sine_part = jnp.sin(angles)[:, None, :]
    lower_half = values_in[..., :half_dim]
    upper_half = values_in[..., half_dim:]
    return jnp.concatenate(
        [
            lower_half * cosine - upper_half * sine_part,
            upper_half * cosine + lower_half * sine_part,
        ],
        axis=-1,
    )


def fill_rows(table, indices, present):
    taken = jnp.take(table, indices.reshape(-1), axis=0)
    return jnp.where(present.reshape(-1)[:, None], taken, jnp.zeros((), table.dtype))


def local(hidden, gain, w_query, w_keyval, lengths, routes):
    rep_count = lax.axis_size("rep")
    seq_count = lax.axis_size("seq")
    x_count = lax.axis_size("x")
    group_size = lax.axis_size("zl")
    z_count = lax.axis_size("zh") * group_size
    tp_count = x_count * z_count
    replica = lax.axis_index("rep")
    seq_index = lax.axis_index("seq")
    sub = lax.axis_index("zl")
    feature_cols = hidden.shape[1]
    local_rows = BUFFER // seq_count
    head_count = w_query.shape[1] // HD
    kv_cols = 2 * HD // group_size
    quarter = HD // 4

    my_lengths = lax.dynamic_index_in_dim(lengths, replica, 0, keepdims=False)
    my_routes = lax.dynamic_index_in_dim(routes, replica, 0, keepdims=False)
    first_block = hidden[:LMAX]
    second_block = lax.dynamic_slice_in_dim(hidden, my_lengths[0], LMAX, 0)
    targets = jnp.arange(rep_count, dtype=jnp.int32)
    outgoing = jnp.where(
        (targets == my_routes[0])[:, None, None], first_block[None], second_block[None]
    ).reshape(rep_count * LMAX, feature_cols)
    slice_cols = quarter // rep_count
    w_half = lax.dynamic_index_in_dim(w_keyval, seq_index, 0, keepdims=False)
    w_half = w_half.reshape(feature_cols, KVH, 2, 2, 2, rep_count, slice_cols)
    w_half = lax.dynamic_index_in_dim(w_half, replica, 5, keepdims=False)
    w_half = w_half.transpose(1, 2, 4, 0, 3, 5).reshape(tp_count, feature_cols, 2 * slice_cols)
    w_mine = lax.all_to_all(w_half, ("x", "zh", "zl"), split_axis=0, concat_axis=0, tiled=True)
    w_spread = jnp.broadcast_to(w_mine[None], (rep_count,) + w_mine.shape)
    w_kv = lax.all_to_all(w_spread, "rep", split_axis=0, concat_axis=0, tiled=True)
    w_kv = w_kv.reshape(rep_count, tp_count, feature_cols, 2, slice_cols).transpose(1, 2, 3, 0, 4)
    incoming = lax.all_to_all(outgoing, "rep", split_axis=0, concat_axis=0, tiled=True)
    w_kv = w_kv.reshape(x_count, z_count, feature_cols, kv_cols)
    tables = response_tables(lengths, routes)
    all_pos = jnp.arange(BUFFER, dtype=jnp.int32)
    segment, within, source_group, pair_first, source = locate(all_pos, replica, tables)
    valid = segment >= 0
    gathered_idx = jnp.where(valid, source_group * LMAX + all_pos - pair_first, 0)
    assembled = fill_rows(incoming, gathered_idx, valid)

    spread = jnp.broadcast_to(assembled[None], (x_count,) + assembled.shape)
    gathered = lax.all_to_all(spread, "x", split_axis=0, concat_axis=0, tiled=True)
    gathered = lax.all_gather(gathered, ("zh", "zl"), axis=0, tiled=False)
    gain_half = lax.dynamic_index_in_dim(
        gain.reshape(seq_count, x_count, z_count, feature_cols), seq_index, 0, keepdims=False
    )
    gathered_f = gathered.astype(jnp.float32)
    scaled = (gathered_f * gain_half.transpose(1, 0, 2)[:, :, None, :]).astype(jnp.bfloat16)
    squares = jnp.sum(gathered_f * gathered_f, axis=(0, 1, 3))
    w_q = w_query.reshape(x_count, z_count, feature_cols, w_query.shape[1])
    query_part = jnp.einsum("zxri,xzic->rc", scaled, w_q, preferred_element_type=jnp.float32)
    kv_part = jnp.einsum("zxri,xzic->rc", scaled, w_kv, preferred_element_type=jnp.float32)

    window = BUFFER - LMIN
    rest = BUFFER - window
    partner = seq_count - 1 - seq_index
    query_cols = query_part.shape[1]
    payload = jnp.concatenate(
        [
            lax.dynamic_slice_in_dim(query_part, partner * local_rows, local_rows, 0).reshape(-1),
            lax.dynamic_slice_in_dim(squares, partner * rest, window),
        ]
    )
    got = lax.ppermute(payload, "seq", perm=[(0, 1), (1, 0)])

    by_window = jnp.stack([kv_part[:window], kv_part[rest:]])
    kv_send = jnp.broadcast_to(
        by_window[:, None], (seq_count, group_size, window, kv_cols)
    ).reshape(seq_count * group_size, window, kv_cols)
    kv_got = lax.all_to_all(kv_send, ("seq", "zl"), split_axis=0, concat_axis=0, tiled=True)
    kv_got = kv_got.reshape(seq_count, group_size, window, kv_cols)
    q_size = local_rows * query_cols
    win_at = seq_index * rest
    query_at = seq_index * local_rows
    query_raw = lax.dynamic_slice_in_dim(query_part, query_at, local_rows, 0) + got[
        :q_size
    ].reshape(local_rows, query_cols)
    own_first = seq_index == 0
    kv_raw = jnp.where(own_first, kv_got[0] + kv_got[1], kv_got[1] + kv_got[0])
    win_squares = lax.dynamic_slice_in_dim(squares, win_at, window) + got[q_size:]
    win_rms = lax.rsqrt(win_squares / D + NORM_EPS)
    query_rms = lax.dynamic_slice_in_dim(win_rms, query_at - win_at, local_rows)

    query_pos = query_at + jnp.arange(local_rows, dtype=jnp.int32)
    query_seg = lax.dynamic_slice_in_dim(segment, query_at, local_rows)
    query_within = lax.dynamic_slice_in_dim(within, query_at, local_rows)
    query_valid = query_seg >= 0
    queries = rotary(
        query_rms[:, None, None] * query_raw.reshape(local_rows, head_count, HD), query_within
    ).astype(jnp.bfloat16)

    key_pos = win_at + jnp.arange(window, dtype=jnp.int32)
    key_seg = lax.dynamic_slice_in_dim(segment, win_at, window)
    key_within = lax.dynamic_slice_in_dim(within, win_at, window)
    kv_scaled = win_rms[None, :, None] * kv_raw
    kv_scaled = kv_scaled.reshape(2, 2, window, 2, quarter).transpose(0, 2, 3, 1, 4)
    key_part = rotary(kv_scaled[0].reshape(window, 1, HD), key_within)[:, 0].astype(jnp.bfloat16)
    value_part = kv_scaled[1].reshape(window, HD).astype(jnp.bfloat16)

    score_scale = 1.0 / math.sqrt(HD)
    allowed = (key_seg[None, :] == query_seg[:, None]) & query_valid[:, None] & (
        key_pos[None, :] <= query_pos[:, None]
    ) | (key_pos[None, :] == query_pos[:, None])
    scores = (
        jnp.einsum("rhd,kd->rhk", queries, key_part, preferred_element_type=jnp.float32)
        * score_scale
    )
    scores = jnp.where(allowed[:, None, :], scores, MASK_FILL)
    new_max = jnp.max(scores, axis=2)
    prob_terms = jnp.where(allowed[:, None, :], jnp.exp(scores - new_max[:, :, None]), 0.0)
    totals = jnp.sum(prob_terms, axis=2)
    accum = jnp.einsum(
        "rhk,kd->rhd",
        prob_terms.astype(jnp.bfloat16),
        value_part,
        preferred_element_type=jnp.float32,
    )
    attended = (
        (accum / totals[:, :, None]).reshape(local_rows, head_count * HD).astype(jnp.bfloat16)
    )
    return jnp.where(query_valid[:, None], attended, jnp.zeros((), jnp.bfloat16))


def solution(mesh):
    heads_per_kv = QH // KVH
    tp_count = mesh.shape["tp"]
    group_size = heads_per_kv * tp_count // QH
    x_count = 4
    z_count = tp_count // x_count
    devices = mesh.devices.reshape(
        mesh.shape["rep"], mesh.shape["seq"], x_count, z_count // group_size, group_size
    )
    grid = jax.sharding.Mesh(devices, ("rep", "seq", "x", "zh", "zl"))
    tp = ("x", "zh", "zl")
    in_specs = (
        P("rep", ("seq",) + tp),
        P(),
        P("seq", tp),
        P(None, tp, None),
        P(),
        P(),
    )
    out_specs = P(("rep", "seq"), tp)
    return jax.shard_map(local, mesh=grid, in_specs=in_specs, out_specs=out_specs, check_vma=False)
```

```python
import math

import jax
import jax.numpy as jnp
from jax import lax
from jax.sharding import PartitionSpec as P

D = 8192
QH = 64
KVH = 8
HD = 128
RESP = 2
LMAX = 192
LMIN = 128
BUFFER = 384


ROPE_BASE = 500000.0
NORM_EPS = 1e-05
MASK_FILL = -1e30


def response_tables(lengths, routes):
    flat_len = lengths.reshape(-1)
    flat_route = routes.reshape(-1)
    response_ids = jnp.arange(flat_len.shape[0], dtype=jnp.int32)
    group_of = response_ids // RESP
    same_route = flat_route[:, None] == flat_route[None, :]
    same_group = group_of[:, None] == group_of[None, :]
    earlier = response_ids[None, :] < response_ids[:, None]
    dest_off = jnp.sum(jnp.where(same_route & earlier, flat_len[None, :], 0), axis=1)
    pair_off = jnp.sum(jnp.where(same_route & same_group & earlier, flat_len[None, :], 0), axis=1)
    src_start = jnp.sum(jnp.where(same_group & earlier, flat_len[None, :], 0), axis=1)
    return (flat_len, flat_route, group_of, dest_off, pair_off, src_start)


def locate(positions, replica, tables):
    flat_len, flat_route, group_of, dest_off, pair_off, src_start = tables
    response_ids = jnp.arange(flat_len.shape[0], dtype=jnp.int32)
    position_col = positions[:, None]
    inside = (
        (flat_route[None, :] == replica)
        & (dest_off[None, :] <= position_col)
        & (position_col < dest_off[None, :] + flat_len[None, :])
    )
    inside_int = inside.astype(jnp.int32)
    segment = jnp.sum(inside_int * (response_ids[None, :] + 1), axis=1) - 1
    seg_start = jnp.sum(inside_int * dest_off[None, :], axis=1)
    source_group = jnp.sum(inside_int * group_of[None, :], axis=1)
    pair_first = jnp.sum(inside_int * (dest_off - pair_off)[None, :], axis=1)
    source = jnp.sum(inside_int * src_start[None, :], axis=1)
    within = jnp.where(segment >= 0, positions - seg_start, 0)
    return (segment, within, source_group, pair_first, source)


def rotary(values_in, within):
    head_dim = values_in.shape[-1]
    half_dim = head_dim // 2
    freq_index = jnp.arange(half_dim, dtype=jnp.float32)
    inverse = jnp.power(ROPE_BASE, -2.0 * freq_index / head_dim)
    angles = within.astype(jnp.float32)[:, None] * inverse[None, :]
    cosine = jnp.cos(angles)[:, None, :]
    sine_part = jnp.sin(angles)[:, None, :]
    lower_half = values_in[..., :half_dim]
    upper_half = values_in[..., half_dim:]
    return jnp.concatenate(
        [
            lower_half * cosine - upper_half * sine_part,
            upper_half * cosine + lower_half * sine_part,
        ],
        axis=-1,
    )


def fill_rows(table, indices, present):
    taken = jnp.take(table, indices.reshape(-1), axis=0)
    return jnp.where(present.reshape(-1)[:, None], taken, jnp.zeros((), table.dtype))


def local(hidden, gain, w_query, w_keyval, lengths, routes):
    rep_count = lax.axis_size("rep")
    seq_count = lax.axis_size("seq")
    x_count = lax.axis_size("x")
    group_size = lax.axis_size("zl")
    z_count = lax.axis_size("zh") * group_size
    tp_count = x_count * z_count
    replica = lax.axis_index("rep")
    seq_index = lax.axis_index("seq")
    sub = lax.axis_index("zl")
    feature_cols = hidden.shape[1]
    local_rows = BUFFER // seq_count
    head_count = w_query.shape[1] // HD
    kv_cols = 2 * HD // group_size
    quarter = HD // 4

    my_lengths = lax.dynamic_index_in_dim(lengths, replica, 0, keepdims=False)
    my_routes = lax.dynamic_index_in_dim(routes, replica, 0, keepdims=False)
    first_block = hidden[:LMAX]
    second_block = lax.dynamic_slice_in_dim(hidden, my_lengths[0], LMAX, 0)
    targets = jnp.arange(rep_count, dtype=jnp.int32)
    outgoing = jnp.where(
        (targets == my_routes[0])[:, None, None], first_block[None], second_block[None]
    ).reshape(rep_count * LMAX, feature_cols)
    slice_cols = quarter // rep_count
    w_half = lax.dynamic_index_in_dim(w_keyval, seq_index, 0, keepdims=False)
    w_half = w_half.reshape(feature_cols, KVH, 2, 2, 2, rep_count, slice_cols)
    w_half = lax.dynamic_index_in_dim(w_half, replica, 5, keepdims=False)
    w_half = w_half.transpose(1, 2, 4, 0, 3, 5).reshape(tp_count, feature_cols, 2 * slice_cols)
    w_mine = lax.all_to_all(w_half, ("x", "zh", "zl"), split_axis=0, concat_axis=0, tiled=True)
    w_spread = jnp.broadcast_to(w_mine[None], (rep_count,) + w_mine.shape)
    w_kv = lax.all_to_all(w_spread, "rep", split_axis=0, concat_axis=0, tiled=True)
    w_kv = w_kv.reshape(rep_count, tp_count, feature_cols, 2, slice_cols).transpose(1, 2, 3, 0, 4)
    incoming = lax.all_to_all(outgoing, "rep", split_axis=0, concat_axis=0, tiled=True)
    w_kv = w_kv.reshape(x_count, z_count, feature_cols, kv_cols)
    tables = response_tables(lengths, routes)
    all_pos = jnp.arange(BUFFER, dtype=jnp.int32)
    segment, within, source_group, pair_first, source = locate(all_pos, replica, tables)
    valid = segment >= 0
    gathered_idx = jnp.where(valid, source_group * LMAX + all_pos - pair_first, 0)
    assembled = fill_rows(incoming, gathered_idx, valid)

    spread = jnp.broadcast_to(assembled[None], (x_count,) + assembled.shape)
    gathered = lax.all_to_all(spread, "x", split_axis=0, concat_axis=0, tiled=True)
    gathered = lax.all_gather(gathered, ("zh", "zl"), axis=0, tiled=False)
    gain_half = lax.dynamic_index_in_dim(
        gain.reshape(seq_count, x_count, z_count, feature_cols), seq_index, 0, keepdims=False
    )
    gathered_f = gathered.astype(jnp.float32)
    scaled = (gathered_f * gain_half.transpose(1, 0, 2)[:, :, None, :]).astype(jnp.bfloat16)
    squares = jnp.sum(gathered_f * gathered_f, axis=(0, 1, 3))
    w_q = w_query.reshape(x_count, z_count, feature_cols, w_query.shape[1])

    def project(first, count, weights):
        rows = lax.dynamic_slice_in_dim(scaled, first, count, 2)
        return jnp.einsum("zxri,xzic->rc", rows, weights, preferred_element_type=jnp.float32)

    window = BUFFER - LMIN
    rest = BUFFER - window
    partner = seq_count - 1 - seq_index
    payload = jnp.concatenate(
        [
            project(partner * local_rows, local_rows, w_q).reshape(-1),
            project(partner * rest, window, w_kv).reshape(-1),
            lax.dynamic_slice_in_dim(squares, partner * rest, window),
        ]
    )
    got = lax.ppermute(payload, "seq", perm=[(0, 1), (1, 0)])
    query_cols = w_q.shape[3]
    q_size = local_rows * query_cols
    kv_size = window * kv_cols
    win_at = seq_index * rest
    query_at = seq_index * local_rows
    query_raw = project(query_at, local_rows, w_q) + got[:q_size].reshape(local_rows, query_cols)
    kv_raw = project(win_at, window, w_kv) + got[q_size : q_size + kv_size].reshape(
        window, kv_cols
    )
    win_squares = lax.dynamic_slice_in_dim(squares, win_at, window) + got[q_size + kv_size :]
    win_rms = lax.rsqrt(win_squares / D + NORM_EPS)
    query_rms = lax.dynamic_slice_in_dim(win_rms, query_at - win_at, local_rows)

    query_pos = query_at + jnp.arange(local_rows, dtype=jnp.int32)
    query_seg = lax.dynamic_slice_in_dim(segment, query_at, local_rows)
    query_within = lax.dynamic_slice_in_dim(within, query_at, local_rows)
    query_valid = query_seg >= 0
    queries = rotary(
        query_rms[:, None, None] * query_raw.reshape(local_rows, head_count, HD), query_within
    ).astype(jnp.bfloat16)

    key_pos = win_at + jnp.arange(window, dtype=jnp.int32)
    key_seg = lax.dynamic_slice_in_dim(segment, win_at, window)
    key_within = lax.dynamic_slice_in_dim(within, win_at, window)
    kv_scaled = (win_rms[:, None] * kv_raw).reshape(window, 2, quarter)
    freq_index = (sub % 2 * quarter + jnp.arange(quarter, dtype=jnp.int32)).astype(jnp.float32)
    inverse = jnp.power(ROPE_BASE, -2.0 * freq_index / HD)
    angles = key_within.astype(jnp.float32)[:, None] * inverse[None, :]
    cosine = jnp.cos(angles)
    sine_part = jnp.sin(angles)
    lower_half = kv_scaled[:, 0]
    upper_half = kv_scaled[:, 1]
    roped = jnp.stack(
        [lower_half * cosine - upper_half * sine_part, upper_half * cosine + lower_half * sine_part],
        axis=1,
    )
    piece = jnp.where(sub < 2, roped, kv_scaled).astype(jnp.bfloat16)
    spread = jnp.broadcast_to(piece[None], (group_size,) + piece.shape)
    pieces = lax.all_to_all(spread, "zl", split_axis=0, concat_axis=0, tiled=True)
    pieces = pieces.reshape(2, 2, window, 2, quarter).transpose(0, 2, 3, 1, 4)
    key_part = pieces[0].reshape(window, HD)
    value_part = pieces[1].reshape(window, HD)

    score_scale = 1.0 / math.sqrt(HD)
    allowed = (key_seg[None, :] == query_seg[:, None]) & query_valid[:, None] & (
        key_pos[None, :] <= query_pos[:, None]
    ) | (key_pos[None, :] == query_pos[:, None])
    scores = (
        jnp.einsum("rhd,kd->rhk", queries, key_part, preferred_element_type=jnp.float32)
        * score_scale
    )
    scores = jnp.where(allowed[:, None, :], scores, MASK_FILL)
    new_max = jnp.max(scores, axis=2)
    prob_terms = jnp.where(allowed[:, None, :], jnp.exp(scores - new_max[:, :, None]), 0.0)
    totals = jnp.sum(prob_terms, axis=2)
    accum = jnp.einsum(
        "rhk,kd->rhd",
        prob_terms.astype(jnp.bfloat16),
        value_part,
        preferred_element_type=jnp.float32,
    )
    attended = (
        (accum / totals[:, :, None]).reshape(local_rows, head_count * HD).astype(jnp.bfloat16)
    )
    return jnp.where(query_valid[:, None], attended, jnp.zeros((), jnp.bfloat16))


def solution(mesh):
    heads_per_kv = QH // KVH
    tp_count = mesh.shape["tp"]
    group_size = heads_per_kv * tp_count // QH
    x_count = 4
    z_count = tp_count // x_count
    devices = mesh.devices.reshape(
        mesh.shape["rep"], mesh.shape["seq"], x_count, z_count // group_size, group_size
    )
    grid = jax.sharding.Mesh(devices, ("rep", "seq", "x", "zh", "zl"))
    tp = ("x", "zh", "zl")
    in_specs = (
        P("rep", ("seq",) + tp),
        P(),
        P("seq", tp),
        P(None, tp, None),
        P(),
        P(),
    )
    out_specs = P(("rep", "seq"), tp)
    return jax.shard_map(local, mesh=grid, in_specs=in_specs, out_specs=out_specs, check_vma=False)
```

```python
import math

import jax
import jax.numpy as jnp
from jax import lax
from jax.sharding import PartitionSpec as P

D = 8192
QH = 64
KVH = 8
HD = 128
RESP = 2
LMAX = 192
LMIN = 128
BUFFER = 384


ROPE_BASE = 500000.0
NORM_EPS = 1e-05
MASK_FILL = -1e30


def response_tables(lengths, routes):
    flat_len = lengths.reshape(-1)
    flat_route = routes.reshape(-1)
    response_ids = jnp.arange(flat_len.shape[0], dtype=jnp.int32)
    group_of = response_ids // RESP
    same_route = flat_route[:, None] == flat_route[None, :]
    same_group = group_of[:, None] == group_of[None, :]
    earlier = response_ids[None, :] < response_ids[:, None]
    dest_off = jnp.sum(jnp.where(same_route & earlier, flat_len[None, :], 0), axis=1)
    pair_off = jnp.sum(jnp.where(same_route & same_group & earlier, flat_len[None, :], 0), axis=1)
    src_start = jnp.sum(jnp.where(same_group & earlier, flat_len[None, :], 0), axis=1)
    return (flat_len, flat_route, group_of, dest_off, pair_off, src_start)


def locate(positions, replica, tables):
    flat_len, flat_route, group_of, dest_off, pair_off, src_start = tables
    response_ids = jnp.arange(flat_len.shape[0], dtype=jnp.int32)
    position_col = positions[:, None]
    inside = (
        (flat_route[None, :] == replica)
        & (dest_off[None, :] <= position_col)
        & (position_col < dest_off[None, :] + flat_len[None, :])
    )
    inside_int = inside.astype(jnp.int32)
    segment = jnp.sum(inside_int * (response_ids[None, :] + 1), axis=1) - 1
    seg_start = jnp.sum(inside_int * dest_off[None, :], axis=1)
    source_group = jnp.sum(inside_int * group_of[None, :], axis=1)
    pair_first = jnp.sum(inside_int * (dest_off - pair_off)[None, :], axis=1)
    source = jnp.sum(inside_int * src_start[None, :], axis=1)
    within = jnp.where(segment >= 0, positions - seg_start, 0)
    return (segment, within, source_group, pair_first, source)


def rotary(values_in, within):
    head_dim = values_in.shape[-1]
    half_dim = head_dim // 2
    freq_index = jnp.arange(half_dim, dtype=jnp.float32)
    inverse = jnp.power(ROPE_BASE, -2.0 * freq_index / head_dim)
    angles = within.astype(jnp.float32)[:, None] * inverse[None, :]
    cosine = jnp.cos(angles)[:, None, :]
    sine_part = jnp.sin(angles)[:, None, :]
    lower_half = values_in[..., :half_dim]
    upper_half = values_in[..., half_dim:]
    return jnp.concatenate(
        [
            lower_half * cosine - upper_half * sine_part,
            upper_half * cosine + lower_half * sine_part,
        ],
        axis=-1,
    )


def fill_rows(table, indices, present):
    taken = jnp.take(table, indices.reshape(-1), axis=0)
    return jnp.where(present.reshape(-1)[:, None], taken, jnp.zeros((), table.dtype))


def local(hidden, gain, w_query, w_keyval, lengths, routes):
    rep_count = lax.axis_size("rep")
    seq_count = lax.axis_size("seq")
    x_count = lax.axis_size("x")
    group_size = lax.axis_size("zl")
    z_count = lax.axis_size("zh") * group_size
    tp_count = x_count * z_count
    replica = lax.axis_index("rep")
    seq_index = lax.axis_index("seq")
    sub = lax.axis_index("zl")
    feature_cols = hidden.shape[1]
    local_rows = BUFFER // seq_count
    head_count = w_query.shape[1] // HD
    kv_cols = 2 * HD // group_size
    quarter = HD // 4

    block = BUFFER - LMIN
    targets = jnp.arange(rep_count, dtype=jnp.int32)
    groups = jnp.arange(routes.shape[0], dtype=jnp.int32)
    to_first = jnp.any(
        (groups[:, None] == replica) & (routes[:, 0][:, None] == targets[None, :]), axis=0
    )
    outgoing = jnp.where(
        to_first[:, None, None], hidden[None, :block], hidden[None, BUFFER - block :]
    ).reshape(rep_count * block, feature_cols)
    slice_cols = quarter // rep_count
    w_half = lax.dynamic_index_in_dim(w_keyval, seq_index, 0, keepdims=False)
    w_half = w_half.reshape(feature_cols, KVH, 2, 2, 2, rep_count, slice_cols)
    w_half = lax.dynamic_index_in_dim(w_half, replica, 5, keepdims=False)
    w_half = w_half.transpose(1, 2, 4, 0, 3, 5).reshape(tp_count, feature_cols, 2 * slice_cols)
    w_mine = lax.all_to_all(w_half, ("x", "zh", "zl"), split_axis=0, concat_axis=0, tiled=True)
    w_spread = jnp.broadcast_to(w_mine[None], (rep_count,) + w_mine.shape)
    w_kv = lax.all_to_all(w_spread, "rep", split_axis=0, concat_axis=0, tiled=True)
    w_kv = w_kv.reshape(rep_count, tp_count, feature_cols, 2, slice_cols).transpose(1, 2, 3, 0, 4)
    incoming = lax.all_to_all(outgoing, "rep", split_axis=0, concat_axis=0, tiled=True)
    w_kv = w_kv.reshape(x_count, z_count, feature_cols, kv_cols)
    tables = response_tables(lengths, routes)
    all_pos = jnp.arange(BUFFER, dtype=jnp.int32)
    segment, within, source_group, pair_first, source = locate(all_pos, replica, tables)
    valid = segment >= 0
    flat_route = tables[1]
    own_route = jnp.take(flat_route, jnp.maximum(segment, 0))
    first_route = jnp.take(flat_route, source_group * RESP)
    block_start = jnp.where(own_route == first_route, 0, BUFFER - block)
    gathered_idx = jnp.where(valid, source_group * block + within + source - block_start, 0)
    assembled = fill_rows(incoming, gathered_idx, valid)

    spread = jnp.broadcast_to(assembled[None], (x_count,) + assembled.shape)
    gathered = lax.all_to_all(spread, "x", split_axis=0, concat_axis=0, tiled=True)
    gathered = lax.all_gather(gathered, ("zh", "zl"), axis=0, tiled=False)
    gain_half = lax.dynamic_index_in_dim(
        gain.reshape(seq_count, x_count, z_count, feature_cols), seq_index, 0, keepdims=False
    )
    gathered_f = gathered.astype(jnp.float32)
    scaled = (gathered_f * gain_half.transpose(1, 0, 2)[:, :, None, :]).astype(jnp.bfloat16)
    squares = jnp.sum(gathered_f * gathered_f, axis=(0, 1, 3))
    w_q = w_query.reshape(x_count, z_count, feature_cols, w_query.shape[1])
    query_part = jnp.einsum("zxri,xzic->rc", scaled, w_q, preferred_element_type=jnp.float32)
    kv_part = jnp.einsum("zxri,xzic->rc", scaled, w_kv, preferred_element_type=jnp.float32)

    window = BUFFER - LMIN
    rest = BUFFER - window
    partner = seq_count - 1 - seq_index
    query_cols = query_part.shape[1]
    payload = jnp.concatenate(
        [
            lax.dynamic_slice_in_dim(query_part, partner * local_rows, local_rows, 0).reshape(-1),
            lax.dynamic_slice_in_dim(kv_part, partner * rest, window, 0).reshape(-1),
            lax.dynamic_slice_in_dim(squares, partner * rest, window),
        ]
    )
    got = lax.ppermute(payload, "seq", perm=[(0, 1), (1, 0)])
    q_size = local_rows * query_cols
    kv_size = window * kv_cols
    win_at = seq_index * rest
    query_at = seq_index * local_rows
    query_raw = lax.dynamic_slice_in_dim(query_part, query_at, local_rows, 0) + got[
        :q_size
    ].reshape(local_rows, query_cols)
    kv_raw = lax.dynamic_slice_in_dim(kv_part, win_at, window, 0) + got[
        q_size : q_size + kv_size
    ].reshape(window, kv_cols)
    win_squares = lax.dynamic_slice_in_dim(squares, win_at, window) + got[q_size + kv_size :]
    win_rms = lax.rsqrt(win_squares / D + NORM_EPS)
    query_rms = lax.dynamic_slice_in_dim(win_rms, query_at - win_at, local_rows)

    query_pos = query_at + jnp.arange(local_rows, dtype=jnp.int32)
    query_seg = lax.dynamic_slice_in_dim(segment, query_at, local_rows)
    query_within = lax.dynamic_slice_in_dim(within, query_at, local_rows)
    query_valid = query_seg >= 0
    queries = rotary(
        query_rms[:, None, None] * query_raw.reshape(local_rows, head_count, HD), query_within
    ).astype(jnp.bfloat16)

    key_pos = win_at + jnp.arange(window, dtype=jnp.int32)
    key_seg = lax.dynamic_slice_in_dim(segment, win_at, window)
    key_within = lax.dynamic_slice_in_dim(within, win_at, window)
    kv_scaled = (win_rms[:, None] * kv_raw).reshape(window, 2, quarter)
    freq_index = (sub % 2 * quarter + jnp.arange(quarter, dtype=jnp.int32)).astype(jnp.float32)
    inverse = jnp.power(ROPE_BASE, -2.0 * freq_index / HD)
    angles = key_within.astype(jnp.float32)[:, None] * inverse[None, :]
    cosine = jnp.cos(angles)
    sine_part = jnp.sin(angles)
    lower_half = kv_scaled[:, 0]
    upper_half = kv_scaled[:, 1]
    roped = jnp.stack(
        [lower_half * cosine - upper_half * sine_part, upper_half * cosine + lower_half * sine_part],
        axis=1,
    )
    piece = jnp.where(sub < 2, roped, kv_scaled).astype(jnp.bfloat16)
    spread = jnp.broadcast_to(piece[None], (group_size,) + piece.shape)
    pieces = lax.all_to_all(spread, "zl", split_axis=0, concat_axis=0, tiled=True)
    pieces = pieces.reshape(2, 2, window, 2, quarter).transpose(0, 2, 3, 1, 4)
    key_part = pieces[0].reshape(window, HD)
    value_part = pieces[1].reshape(window, HD)

    score_scale = 1.0 / math.sqrt(HD)
    allowed = (key_seg[None, :] == query_seg[:, None]) & query_valid[:, None] & (
        key_pos[None, :] <= query_pos[:, None]
    ) | (key_pos[None, :] == query_pos[:, None])
    scores = (
        jnp.einsum("rhd,kd->rhk", queries, key_part, preferred_element_type=jnp.float32)
        * score_scale
    )
    scores = jnp.where(allowed[:, None, :], scores, MASK_FILL)
    new_max = jnp.max(scores, axis=2)
    prob_terms = jnp.where(allowed[:, None, :], jnp.exp(scores - new_max[:, :, None]), 0.0)
    totals = jnp.sum(prob_terms, axis=2)
    accum = jnp.einsum(
        "rhk,kd->rhd",
        prob_terms.astype(jnp.bfloat16),
        value_part,
        preferred_element_type=jnp.float32,
    )
    attended = (
        (accum / totals[:, :, None]).reshape(local_rows, head_count * HD).astype(jnp.bfloat16)
    )
    return jnp.where(query_valid[:, None], attended, jnp.zeros((), jnp.bfloat16))


def solution(mesh):
    heads_per_kv = QH // KVH
    tp_count = mesh.shape["tp"]
    group_size = heads_per_kv * tp_count // QH
    x_count = 4
    z_count = tp_count // x_count
    devices = mesh.devices.reshape(
        mesh.shape["rep"], mesh.shape["seq"], x_count, z_count // group_size, group_size
    )
    grid = jax.sharding.Mesh(devices, ("rep", "seq", "x", "zh", "zl"))
    tp = ("x", "zh", "zl")
    in_specs = (
        P("rep", ("seq",) + tp),
        P(),
        P("seq", tp),
        P(None, tp, None),
        P(),
        P(),
    )
    out_specs = P(("rep", "seq"), tp)
    return jax.shard_map(local, mesh=grid, in_specs=in_specs, out_specs=out_specs, check_vma=False)
```

```python
import math

import jax
import jax.numpy as jnp
from jax import lax
from jax.sharding import PartitionSpec as P

D = 8192
QH = 64
KVH = 8
HD = 128
RESP = 2
LMAX = 192
LMIN = 128
BUFFER = 384


ROPE_BASE = 500000.0
NORM_EPS = 1e-05
MASK_FILL = -1e30


def response_tables(lengths, routes):
    flat_len = lengths.reshape(-1)
    flat_route = routes.reshape(-1)
    response_ids = jnp.arange(flat_len.shape[0], dtype=jnp.int32)
    group_of = response_ids // RESP
    same_route = flat_route[:, None] == flat_route[None, :]
    same_group = group_of[:, None] == group_of[None, :]
    earlier = response_ids[None, :] < response_ids[:, None]
    dest_off = jnp.sum(jnp.where(same_route & earlier, flat_len[None, :], 0), axis=1)
    pair_off = jnp.sum(jnp.where(same_route & same_group & earlier, flat_len[None, :], 0), axis=1)
    src_start = jnp.sum(jnp.where(same_group & earlier, flat_len[None, :], 0), axis=1)
    return (flat_len, flat_route, group_of, dest_off, pair_off, src_start)


def locate(positions, replica, tables):
    flat_len, flat_route, group_of, dest_off, pair_off, src_start = tables
    response_ids = jnp.arange(flat_len.shape[0], dtype=jnp.int32)
    position_col = positions[:, None]
    inside = (
        (flat_route[None, :] == replica)
        & (dest_off[None, :] <= position_col)
        & (position_col < dest_off[None, :] + flat_len[None, :])
    )
    inside_int = inside.astype(jnp.int32)
    segment = jnp.sum(inside_int * (response_ids[None, :] + 1), axis=1) - 1
    seg_start = jnp.sum(inside_int * dest_off[None, :], axis=1)
    source_group = jnp.sum(inside_int * group_of[None, :], axis=1)
    pair_first = jnp.sum(inside_int * (dest_off - pair_off)[None, :], axis=1)
    source = jnp.sum(inside_int * src_start[None, :], axis=1)
    within = jnp.where(segment >= 0, positions - seg_start, 0)
    return (segment, within, source_group, pair_first, source)


def rotary(values_in, within):
    head_dim = values_in.shape[-1]
    half_dim = head_dim // 2
    freq_index = jnp.arange(half_dim, dtype=jnp.float32)
    inverse = jnp.power(ROPE_BASE, -2.0 * freq_index / head_dim)
    angles = within.astype(jnp.float32)[:, None] * inverse[None, :]
    cosine = jnp.cos(angles)[:, None, :]
    sine_part = jnp.sin(angles)[:, None, :]
    lower_half = values_in[..., :half_dim]
    upper_half = values_in[..., half_dim:]
    return jnp.concatenate(
        [
            lower_half * cosine - upper_half * sine_part,
            upper_half * cosine + lower_half * sine_part,
        ],
        axis=-1,
    )


def fill_rows(table, indices, present):
    taken = jnp.take(table, indices.reshape(-1), axis=0)
    return jnp.where(present.reshape(-1)[:, None], taken, jnp.zeros((), table.dtype))


def local(hidden, gain, w_query, w_keyval, lengths, routes):
    rep_count = lax.axis_size("rep")
    seq_count = lax.axis_size("seq")
    x_count = lax.axis_size("x")
    group_size = lax.axis_size("zl")
    z_count = lax.axis_size("zh") * group_size
    tp_count = x_count * z_count
    replica = lax.axis_index("rep")
    seq_index = lax.axis_index("seq")
    sub = lax.axis_index("zl")
    feature_cols = hidden.shape[1]
    local_rows = BUFFER // seq_count
    head_count = w_query.shape[1] // HD
    kv_cols = 2 * HD // group_size
    quarter = HD // 4

    block = BUFFER - LMIN
    targets = jnp.arange(rep_count, dtype=jnp.int32)
    groups = jnp.arange(routes.shape[0], dtype=jnp.int32)
    to_first = jnp.any(
        (groups[:, None] == replica) & (routes[:, 0][:, None] == targets[None, :]), axis=0
    )
    outgoing = jnp.where(
        to_first[:, None, None], hidden[None, :block], hidden[None, BUFFER - block :]
    ).reshape(rep_count * block, feature_cols)
    slice_cols = quarter // rep_count
    w_half = lax.dynamic_index_in_dim(w_keyval, seq_index, 0, keepdims=False)
    w_half = w_half.reshape(feature_cols, KVH, 2, 2, 2, rep_count, slice_cols)
    w_half = lax.dynamic_index_in_dim(w_half, replica, 5, keepdims=False)
    w_half = w_half.transpose(1, 2, 4, 0, 3, 5).reshape(tp_count, feature_cols, 2 * slice_cols)
    w_mine = lax.all_to_all(w_half, ("x", "zh", "zl"), split_axis=0, concat_axis=0, tiled=True)
    w_spread = jnp.broadcast_to(w_mine[None], (rep_count,) + w_mine.shape)
    w_kv = lax.all_to_all(w_spread, "rep", split_axis=0, concat_axis=0, tiled=True)
    w_kv = w_kv.reshape(rep_count, tp_count, feature_cols, 2, slice_cols).transpose(1, 2, 3, 0, 4)
    incoming = lax.all_to_all(outgoing, "rep", split_axis=0, concat_axis=0, tiled=True)
    w_kv = w_kv.reshape(x_count, z_count, feature_cols, kv_cols)
    tables = response_tables(lengths, routes)
    all_pos = jnp.arange(BUFFER, dtype=jnp.int32)
    segment, within, source_group, pair_first, source = locate(all_pos, replica, tables)
    valid = segment >= 0
    flat_len, flat_route, group_of, dest_off, pair_off, src_start = tables
    block_start = jnp.where(routes == routes[:, :1], 0, BUFFER - block).reshape(-1)
    inside = (
        (flat_route[None, :] == replica)
        & (dest_off[None, :] <= all_pos[:, None])
        & (all_pos[:, None] < (dest_off + flat_len)[None, :])
    )
    shift = jnp.sum(inside.astype(jnp.int32) * (src_start - block_start)[None, :], axis=1)
    gathered_idx = jnp.where(valid, source_group * block + within + shift, 0)
    assembled = fill_rows(incoming, gathered_idx, valid)

    spread = jnp.broadcast_to(assembled[None], (x_count,) + assembled.shape)
    gathered = lax.all_to_all(spread, "x", split_axis=0, concat_axis=0, tiled=True)
    gathered = lax.all_gather(gathered, ("zh", "zl"), axis=0, tiled=False)
    gain_half = lax.dynamic_index_in_dim(
        gain.reshape(seq_count, x_count, z_count, feature_cols), seq_index, 0, keepdims=False
    )
    gathered_f = gathered.astype(jnp.float32)
    scaled = (gathered_f * gain_half.transpose(1, 0, 2)[:, :, None, :]).astype(jnp.bfloat16)
    squares = jnp.sum(gathered_f * gathered_f, axis=(0, 1, 3))
    w_q = w_query.reshape(x_count, z_count, feature_cols, w_query.shape[1])
    query_part = jnp.einsum("zxri,xzic->rc", scaled, w_q, preferred_element_type=jnp.float32)
    kv_part = jnp.einsum("zxri,xzic->rc", scaled, w_kv, preferred_element_type=jnp.float32)

    window = BUFFER - LMIN
    rest = BUFFER - window
    partner = seq_count - 1 - seq_index
    query_cols = query_part.shape[1]
    payload = jnp.concatenate(
        [
            lax.dynamic_slice_in_dim(query_part, partner * local_rows, local_rows, 0).reshape(-1),
            lax.dynamic_slice_in_dim(kv_part, partner * rest, window, 0).reshape(-1),
            lax.dynamic_slice_in_dim(squares, partner * rest, window),
        ]
    )
    got = lax.ppermute(payload, "seq", perm=[(0, 1), (1, 0)])
    q_size = local_rows * query_cols
    kv_size = window * kv_cols
    win_at = seq_index * rest
    query_at = seq_index * local_rows
    query_raw = lax.dynamic_slice_in_dim(query_part, query_at, local_rows, 0) + got[
        :q_size
    ].reshape(local_rows, query_cols)
    kv_raw = lax.dynamic_slice_in_dim(kv_part, win_at, window, 0) + got[
        q_size : q_size + kv_size
    ].reshape(window, kv_cols)
    win_squares = lax.dynamic_slice_in_dim(squares, win_at, window) + got[q_size + kv_size :]
    win_rms = lax.rsqrt(win_squares / D + NORM_EPS)
    query_rms = lax.dynamic_slice_in_dim(win_rms, query_at - win_at, local_rows)

    query_pos = query_at + jnp.arange(local_rows, dtype=jnp.int32)
    query_seg = lax.dynamic_slice_in_dim(segment, query_at, local_rows)
    query_within = lax.dynamic_slice_in_dim(within, query_at, local_rows)
    query_valid = query_seg >= 0
    queries = rotary(
        query_rms[:, None, None] * query_raw.reshape(local_rows, head_count, HD), query_within
    ).astype(jnp.bfloat16)

    key_pos = win_at + jnp.arange(window, dtype=jnp.int32)
    key_seg = lax.dynamic_slice_in_dim(segment, win_at, window)
    key_within = lax.dynamic_slice_in_dim(within, win_at, window)
    kv_scaled = (win_rms[:, None] * kv_raw).reshape(window, 2, quarter)
    freq_index = (sub % 2 * quarter + jnp.arange(quarter, dtype=jnp.int32)).astype(jnp.float32)
    inverse = jnp.power(ROPE_BASE, -2.0 * freq_index / HD)
    angles = key_within.astype(jnp.float32)[:, None] * inverse[None, :]
    cosine = jnp.cos(angles)
    sine_part = jnp.sin(angles)
    lower_half = kv_scaled[:, 0]
    upper_half = kv_scaled[:, 1]
    roped = jnp.stack(
        [lower_half * cosine - upper_half * sine_part, upper_half * cosine + lower_half * sine_part],
        axis=1,
    )
    piece = jnp.where(sub < 2, roped, kv_scaled).astype(jnp.bfloat16)
    spread = jnp.broadcast_to(piece[None], (group_size,) + piece.shape)
    pieces = lax.all_to_all(spread, "zl", split_axis=0, concat_axis=0, tiled=True)
    pieces = pieces.reshape(2, 2, window, 2, quarter).transpose(0, 2, 3, 1, 4)
    key_part = pieces[0].reshape(window, HD)
    value_part = pieces[1].reshape(window, HD)

    score_scale = 1.0 / math.sqrt(HD)
    allowed = (key_seg[None, :] == query_seg[:, None]) & query_valid[:, None] & (
        key_pos[None, :] <= query_pos[:, None]
    ) | (key_pos[None, :] == query_pos[:, None])
    scores = (
        jnp.einsum("rhd,kd->rhk", queries, key_part, preferred_element_type=jnp.float32)
        * score_scale
    )
    scores = jnp.where(allowed[:, None, :], scores, MASK_FILL)
    new_max = jnp.max(scores, axis=2)
    prob_terms = jnp.where(allowed[:, None, :], jnp.exp(scores - new_max[:, :, None]), 0.0)
    totals = jnp.sum(prob_terms, axis=2)
    accum = jnp.einsum(
        "rhk,kd->rhd",
        prob_terms.astype(jnp.bfloat16),
        value_part,
        preferred_element_type=jnp.float32,
    )
    attended = (
        (accum / totals[:, :, None]).reshape(local_rows, head_count * HD).astype(jnp.bfloat16)
    )
    return jnp.where(query_valid[:, None], attended, jnp.zeros((), jnp.bfloat16))


def solution(mesh):
    heads_per_kv = QH // KVH
    tp_count = mesh.shape["tp"]
    group_size = heads_per_kv * tp_count // QH
    x_count = 4
    z_count = tp_count // x_count
    devices = mesh.devices.reshape(
        mesh.shape["rep"], mesh.shape["seq"], x_count, z_count // group_size, group_size
    )
    grid = jax.sharding.Mesh(devices, ("rep", "seq", "x", "zh", "zl"))
    tp = ("x", "zh", "zl")
    in_specs = (
        P("rep", ("seq",) + tp),
        P(),
        P("seq", tp),
        P(None, tp, None),
        P(),
        P(),
    )
    out_specs = P(("rep", "seq"), tp)
    return jax.shard_map(local, mesh=grid, in_specs=in_specs, out_specs=out_specs, check_vma=False)
```

```python
import math

import jax
import jax.numpy as jnp
from jax import lax
from jax.sharding import PartitionSpec as P

D = 8192
QH = 64
KVH = 8
HD = 128
RESP = 2
LMAX = 192
LMIN = 128
BUFFER = 384


ROPE_BASE = 500000.0
NORM_EPS = 1e-05
MASK_FILL = -1e30


def response_tables(lengths, routes):
    flat_len = lengths.reshape(-1)
    flat_route = routes.reshape(-1)
    response_ids = jnp.arange(flat_len.shape[0], dtype=jnp.int32)
    group_of = response_ids // RESP
    same_route = flat_route[:, None] == flat_route[None, :]
    same_group = group_of[:, None] == group_of[None, :]
    earlier = response_ids[None, :] < response_ids[:, None]
    dest_off = jnp.sum(jnp.where(same_route & earlier, flat_len[None, :], 0), axis=1)
    pair_off = jnp.sum(jnp.where(same_route & same_group & earlier, flat_len[None, :], 0), axis=1)
    src_start = jnp.sum(jnp.where(same_group & earlier, flat_len[None, :], 0), axis=1)
    return (flat_len, flat_route, group_of, dest_off, pair_off, src_start)


def locate(positions, replica, tables):
    flat_len, flat_route, group_of, dest_off, pair_off, src_start = tables
    response_ids = jnp.arange(flat_len.shape[0], dtype=jnp.int32)
    position_col = positions[:, None]
    inside = (
        (flat_route[None, :] == replica)
        & (dest_off[None, :] <= position_col)
        & (position_col < dest_off[None, :] + flat_len[None, :])
    )
    inside_int = inside.astype(jnp.int32)
    segment = jnp.sum(inside_int * (response_ids[None, :] + 1), axis=1) - 1
    seg_start = jnp.sum(inside_int * dest_off[None, :], axis=1)
    source_group = jnp.sum(inside_int * group_of[None, :], axis=1)
    pair_first = jnp.sum(inside_int * (dest_off - pair_off)[None, :], axis=1)
    source = jnp.sum(inside_int * src_start[None, :], axis=1)
    within = jnp.where(segment >= 0, positions - seg_start, 0)
    return (segment, within, source_group, pair_first, source)


def rotary(values_in, within):
    head_dim = values_in.shape[-1]
    half_dim = head_dim // 2
    freq_index = jnp.arange(half_dim, dtype=jnp.float32)
    inverse = jnp.power(ROPE_BASE, -2.0 * freq_index / head_dim)
    angles = within.astype(jnp.float32)[:, None] * inverse[None, :]
    cosine = jnp.cos(angles)[:, None, :]
    sine_part = jnp.sin(angles)[:, None, :]
    lower_half = values_in[..., :half_dim]
    upper_half = values_in[..., half_dim:]
    return jnp.concatenate(
        [
            lower_half * cosine - upper_half * sine_part,
            upper_half * cosine + lower_half * sine_part,
        ],
        axis=-1,
    )


def fill_rows(table, indices, present):
    taken = jnp.take(table, indices.reshape(-1), axis=0)
    return jnp.where(present.reshape(-1)[:, None], taken, jnp.zeros((), table.dtype))


def local(hidden, gain, w_query, w_keyval, lengths, routes):
    rep_count = lax.axis_size("rep")
    seq_count = lax.axis_size("seq")
    x_count = lax.axis_size("x")
    group_size = lax.axis_size("zl")
    z_count = lax.axis_size("zh") * group_size
    tp_count = x_count * z_count
    replica = lax.axis_index("rep")
    seq_index = lax.axis_index("seq")
    sub = lax.axis_index("zl")
    feature_cols = hidden.shape[1]
    local_rows = BUFFER // seq_count
    head_count = w_query.shape[1] // HD
    kv_cols = 2 * HD // group_size
    quarter = HD // 4

    block = BUFFER - LMIN
    targets = jnp.arange(rep_count, dtype=jnp.int32)
    groups = jnp.arange(routes.shape[0], dtype=jnp.int32)
    to_first = jnp.any(
        (groups[:, None] == replica) & (routes[:, 0][:, None] == targets[None, :]), axis=0
    )
    outgoing = jnp.where(
        to_first[:, None, None], hidden[None, :block], hidden[None, BUFFER - block :]
    ).reshape(rep_count * block, feature_cols)
    slice_cols = quarter // rep_count
    w_half = lax.dynamic_index_in_dim(w_keyval, seq_index, 0, keepdims=False)
    w_half = w_half.reshape(feature_cols, KVH, 2, 2, 2, rep_count, slice_cols)
    w_half = lax.dynamic_index_in_dim(w_half, replica, 5, keepdims=False)
    w_half = w_half.transpose(1, 2, 4, 0, 3, 5).reshape(tp_count, feature_cols, 2 * slice_cols)
    w_mine = lax.all_to_all(w_half, ("x", "zh", "zl"), split_axis=0, concat_axis=0, tiled=True)
    w_spread = jnp.broadcast_to(w_mine[None], (rep_count,) + w_mine.shape)
    w_kv = lax.all_to_all(w_spread, "rep", split_axis=0, concat_axis=0, tiled=True)
    w_kv = w_kv.reshape(rep_count, tp_count, feature_cols, 2, slice_cols).transpose(1, 2, 3, 0, 4)
    incoming = lax.all_to_all(outgoing, "rep", split_axis=0, concat_axis=0, tiled=True)
    w_kv = w_kv.reshape(x_count, z_count, feature_cols, kv_cols)
    tables = response_tables(lengths, routes)
    all_pos = jnp.arange(BUFFER, dtype=jnp.int32)
    segment, within, source_group, pair_first, source = locate(all_pos, replica, tables)
    valid = segment >= 0
    flat_len, flat_route, group_of, dest_off, pair_off, src_start = tables
    block_start = jnp.where(routes == routes[:, :1], 0, BUFFER - block).reshape(-1)
    inside = (
        (flat_route[None, :] == replica)
        & (dest_off[None, :] <= all_pos[:, None])
        & (all_pos[:, None] < (dest_off + flat_len)[None, :])
    )
    shift = jnp.sum(inside.astype(jnp.int32) * (src_start - block_start)[None, :], axis=1)
    gathered_idx = jnp.where(valid, source_group * block + within + shift, 0)
    assembled = fill_rows(incoming, gathered_idx, valid)

    spread = jnp.broadcast_to(assembled[None], (x_count,) + assembled.shape)
    gathered = lax.all_to_all(spread, "x", split_axis=0, concat_axis=0, tiled=True)
    gathered = lax.all_gather(gathered, ("zh", "zl"), axis=0, tiled=False)
    gain_half = lax.dynamic_index_in_dim(
        gain.reshape(seq_count, x_count, z_count, feature_cols), seq_index, 0, keepdims=False
    )
    gathered_f = gathered.astype(jnp.float32)
    scaled = (gathered_f * gain_half.transpose(1, 0, 2)[:, :, None, :]).astype(jnp.bfloat16)
    squares = jnp.sum(gathered_f * gathered_f, axis=(0, 1, 3))
    w_q = w_query.reshape(x_count, z_count, feature_cols, w_query.shape[1])
    query_part = jnp.einsum("zxri,xzic->rc", scaled, w_q, preferred_element_type=jnp.float32)
    kv_part = jnp.einsum("zxri,xzic->rc", scaled, w_kv, preferred_element_type=jnp.float32)

    window = BUFFER - LMIN
    rest = BUFFER - window
    partner = seq_count - 1 - seq_index
    query_cols = query_part.shape[1]
    payload = jnp.concatenate(
        [
            lax.dynamic_slice_in_dim(query_part, partner * local_rows, local_rows, 0),
            lax.dynamic_slice_in_dim(kv_part, partner * rest, window, 0).reshape(-1, query_cols),
            lax.dynamic_slice_in_dim(squares, partner * rest, window).reshape(-1, query_cols),
        ],
        axis=0,
    )
    got = lax.ppermute(payload, "seq", perm=[(0, 1), (1, 0)])
    kv_rows = window * kv_cols // query_cols
    win_at = seq_index * rest
    query_at = seq_index * local_rows
    query_raw = lax.dynamic_slice_in_dim(query_part, query_at, local_rows, 0) + got[:local_rows]
    kv_raw = lax.dynamic_slice_in_dim(kv_part, win_at, window, 0) + got[
        local_rows : local_rows + kv_rows
    ].reshape(window, kv_cols)
    win_squares = lax.dynamic_slice_in_dim(squares, win_at, window) + got[
        local_rows + kv_rows :
    ].reshape(-1)
    win_rms = lax.rsqrt(win_squares / D + NORM_EPS)
    query_rms = lax.dynamic_slice_in_dim(win_rms, query_at - win_at, local_rows)

    query_pos = query_at + jnp.arange(local_rows, dtype=jnp.int32)
    query_seg = lax.dynamic_slice_in_dim(segment, query_at, local_rows)
    query_within = lax.dynamic_slice_in_dim(within, query_at, local_rows)
    query_valid = query_seg >= 0
    queries = rotary(
        query_rms[:, None, None] * query_raw.reshape(local_rows, head_count, HD), query_within
    ).astype(jnp.bfloat16)

    key_pos = win_at + jnp.arange(window, dtype=jnp.int32)
    key_seg = lax.dynamic_slice_in_dim(segment, win_at, window)
    key_within = lax.dynamic_slice_in_dim(within, win_at, window)
    kv_scaled = (win_rms[:, None] * kv_raw).reshape(window, 2, quarter)
    freq_index = (sub % 2 * quarter + jnp.arange(quarter, dtype=jnp.int32)).astype(jnp.float32)
    inverse = jnp.power(ROPE_BASE, -2.0 * freq_index / HD)
    angles = key_within.astype(jnp.float32)[:, None] * inverse[None, :]
    cosine = jnp.cos(angles)
    sine_part = jnp.sin(angles)
    lower_half = kv_scaled[:, 0]
    upper_half = kv_scaled[:, 1]
    roped = jnp.stack(
        [lower_half * cosine - upper_half * sine_part, upper_half * cosine + lower_half * sine_part],
        axis=1,
    )
    piece = jnp.where(sub < 2, roped, kv_scaled).astype(jnp.bfloat16)
    spread = jnp.broadcast_to(piece[None], (group_size,) + piece.shape)
    pieces = lax.all_to_all(spread, "zl", split_axis=0, concat_axis=0, tiled=True)
    pieces = pieces.reshape(2, 2, window, 2, quarter).transpose(0, 2, 3, 1, 4)
    key_part = pieces[0].reshape(window, HD)
    value_part = pieces[1].reshape(window, HD)

    score_scale = 1.0 / math.sqrt(HD)
    allowed = (key_seg[None, :] == query_seg[:, None]) & query_valid[:, None] & (
        key_pos[None, :] <= query_pos[:, None]
    ) | (key_pos[None, :] == query_pos[:, None])
    scores = (
        jnp.einsum("rhd,kd->rhk", queries, key_part, preferred_element_type=jnp.float32)
        * score_scale
    )
    scores = jnp.where(allowed[:, None, :], scores, MASK_FILL)
    new_max = jnp.max(scores, axis=2)
    prob_terms = jnp.where(allowed[:, None, :], jnp.exp(scores - new_max[:, :, None]), 0.0)
    totals = jnp.sum(prob_terms, axis=2)
    accum = jnp.einsum(
        "rhk,kd->rhd",
        prob_terms.astype(jnp.bfloat16),
        value_part,
        preferred_element_type=jnp.float32,
    )
    attended = (
        (accum / totals[:, :, None]).reshape(local_rows, head_count * HD).astype(jnp.bfloat16)
    )
    return jnp.where(query_valid[:, None], attended, jnp.zeros((), jnp.bfloat16))


def solution(mesh):
    heads_per_kv = QH // KVH
    tp_count = mesh.shape["tp"]
    group_size = heads_per_kv * tp_count // QH
    x_count = 4
    z_count = tp_count // x_count
    devices = mesh.devices.reshape(
        mesh.shape["rep"], mesh.shape["seq"], x_count, z_count // group_size, group_size
    )
    grid = jax.sharding.Mesh(devices, ("rep", "seq", "x", "zh", "zl"))
    tp = ("x", "zh", "zl")
    in_specs = (
        P("rep", ("seq",) + tp),
        P(),
        P("seq", tp),
        P(None, tp, None),
        P(),
        P(),
    )
    out_specs = P(("rep", "seq"), tp)
    return jax.shard_map(local, mesh=grid, in_specs=in_specs, out_specs=out_specs, check_vma=False)
```
